256 devices in a mesh: section: 4 (over y), expert: 64 (over z, x, core).
Axes of the slice: x: 4, y: 4, z: 8, core: 2. Of those that a mesh axis runs over, the one named last changes fastest.
Arguments:
- in_flight: bfloat16 [4, 4096, 2048], P('section', 'expert'), may hold values from -6 to 6
- entering: bfloat16 [1, 4096, 2048], P(None, 'expert'), may hold values from -6 to 6
- norm_gain: bfloat16 [4, 2048], P('section'), may hold values from 0.5 to 1.5
- w_gate: bfloat16 [4, 64, 2048, 768], P('section', 'expert'), may hold values from -0.125 to 0.125
- w_up: bfloat16 [4, 64, 2048, 768], P('section', 'expert'), may hold values from -0.125 to 0.125
- w_down: bfloat16 [4, 64, 768, 2048], P('section', 'expert'), may hold values from -0.21875 to 0.21875
- routes: int32 [4, 2, 4096, 8], P('section', None, 'expert'), may hold values from 0 to 63, all different within a row; in each aligned block of 32 rows (0 to 31, 32 to 63, ..., all dimensions but the last counted through in order) at most 6 rows name the same one
- combine_weight: float32 [4, 2, 4096, 8], P('section', None, 'expert'), may hold values from 0.2 to 0.6
Outputs:
- trace: bfloat16 [2, 4, 4096, 2048], P(None, 'section', 'expert')
The draws below stay inside these ranges and needn't reach their ends.
Inputs may be any that keep to these rules, and one draw needn't show every extreme that they name: `routes`: each row names 8 different experts. In each aligned block of 32 rows (all leading dimensions taken together, in order) no expert is named by more than 6 rows, a bound that some block reaches.
All inputs are finite; a program needn't handle non-finite values.
Results may differ from the reference program's by a relative error of at most 0.0085.
Values may be sent and summed in bfloat16 or wider, within the bound.
No kernel may reach another device: no remote copies, remote signals or barrier semaphores. Data moves between devices by JAX's collectives and lax.ppermute only.
A program may use at most 128 MiB of HBM per device.

```python
import math
import jax
import jax.numpy as jnp
import numpy as np
from jax import lax

D = 2048
FF = 768
TOPK = 8
TICKS = 2
LAYERS = 4
EXPERTS = 64
TOKENS = 4096
TOK_HALF = 32
CAP = 6
N_EXPERT = 64


def block_levels(stream_key, shape, cuts, smallest, high):
    def one(axis_at, shards_of):
        heights = jax.random.uniform(jax.random.fold_in(jax.random.fold_in(stream_key, 6), axis_at), (shards_of,), jnp.float32, smallest / len(cuts), high / len(cuts))
        return jnp.repeat(jnp.exp(heights), shape[axis_at] // shards_of).reshape((-1,) + (1,) * (len(shape) - axis_at - 1))

    loudness = one(*cuts[0])
    for cut in cuts[1:]:
        loudness = loudness * one(*cut)
    return loudness


def shared_out(stream_key, own, number, rows, number_of, top, bound, skew):
    ranking = jax.random.permutation(stream_key, number_of)
    crowded, usual = load_shares(number_of, rows * top, bound, skew, True), load_shares(number_of, rows * top, bound, skew, False)
    places = jnp.arange(number_of)

    def named(tallies, turn):
        used = int((tallies > 0).sum())
        fixed = max(1, used // 4)
        shifted = fixed + (places - fixed + turn * (used - fixed)) % max(1, number_of - fixed)
        return jnp.zeros((number_of,), jnp.int32).at[ranking[jnp.where(places < fixed, places, shifted)]].set(jnp.asarray(tallies, jnp.int32))

    tallies = jnp.where(number % 4 == 0, named(crowded, number // 4), named(usual, number - number // 4 - 1))
    mixed = jax.random.permutation(jax.random.fold_in(own, 3), number_of)
    source_of, receiver = mixed[0:number_of // 2 * 2:2], mixed[1:number_of // 2 * 2:2]
    room = jnp.minimum(tallies[source_of] - 1, bound - tallies[receiver]) // 2
    room = jnp.where((source_of == ranking[0]) | (receiver == ranking[0]) | (tallies[receiver] == 0), 0, jnp.maximum(room, 0))
    shifted = jax.random.randint(jax.random.fold_in(own, 4), (number_of // 2,), 0, 1 << 20) % (room + 1)
    tallies = tallies.at[source_of].add(-shifted).at[receiver].add(shifted)
    members = jnp.searchsorted(jnp.cumsum(tallies), jnp.arange(rows * top), side="right").astype(jnp.int32)
    table = members.reshape(top, rows).T
    table = table[jax.random.permutation(jax.random.fold_in(own, 1), rows)]
    turn = jax.random.randint(jax.random.fold_in(own, 2), (rows, 1), 0, top)
    return jnp.take_along_axis(table, (jnp.arange(top)[None, :] + turn) % top, axis=1)


def load_shares(count, total, bound, slope, full):
    loads = [(1 << 20) // math.isqrt(rank ** slope) + 1 for rank in range(1, count + 1)]
    largest = bound if full else min(bound, max(-(-total // count), total * loads[0] // sum(loads)))
    least = 1 if total - largest >= count - 1 else 0
    counts, surplus = [largest] + [least] * (count - 1), total - largest - least * (count - 1)
    while surplus > 0:
        candidates = [i for i in range(1, count) if counts[i] < largest] or [i for i in range(1, count) if counts[i] < bound]
        mass, budget = sum([loads[i] for i in candidates]), surplus
        for i in candidates:
            extra = min(bound - counts[i], max(1, budget * loads[i] // mass), surplus)
            counts[i] = counts[i] + extra
            surplus = surplus - extra
    return np.array(counts)


def gaussian(key, dims, scale, most, cuts=(), held_as=jnp.bfloat16):
    values = jax.random.normal(key, dims, jnp.float32) * scale
    if len(cuts) > 0:
        values = block_levels(key, dims, cuts, -0.22, 0.18) * values
    return jnp.clip(values, min=-most, max=most).astype(held_as)


def setup_inputs(seed: int = 0) -> dict:
    streams_of = jax.random.split(jax.random.key(seed), 9)
    in_flight = gaussian(streams_of[0], (LAYERS, TOKENS, D), 1.0, 6.0, ((0, 4), (1, 64)))
    entering = gaussian(streams_of[1], (TICKS - 1, TOKENS, D), 1.0, 6.0, ((1, 64),))
    norm_gain = jnp.clip(1.0 + 0.1 * jax.random.normal(streams_of[2], (LAYERS, D), jnp.float32), 0.5, 1.5).astype(jnp.bfloat16)
    w_gate = gaussian(streams_of[3], (LAYERS, EXPERTS, D, FF), D ** -0.5, 0.125, ((0, 4), (1, 64)))
    w_up = gaussian(streams_of[4], (LAYERS, EXPERTS, D, FF), D ** -0.5, 0.125, ((0, 4), (1, 64)))
    w_down = gaussian(streams_of[5], (LAYERS, EXPERTS, FF, D), FF ** -0.5, 0.21875, ((0, 4), (1, 64)))
    routes_keys = jax.random.split(jax.random.fold_in(streams_of[6], 1), LAYERS * TICKS * TOKENS // TOK_HALF)
    routes_turns = jax.random.permutation(jax.random.fold_in(streams_of[6], 3), LAYERS * TICKS * TOKENS // TOK_HALF)
    routes = jax.vmap(lambda own, number: shared_out(jax.random.fold_in(streams_of[6], 2), own, number, TOK_HALF, EXPERTS, TOPK, CAP, 1))(routes_keys, routes_turns).reshape((LAYERS, TICKS, TOKENS, TOPK))
    combine_weight = jnp.clip(0.2 + 0.400000021 * jax.random.uniform(streams_of[7], (LAYERS, TICKS, TOKENS, TOPK), jnp.float32) ** block_levels(streams_of[7], (LAYERS, TICKS, TOKENS, TOPK), ((0, 4), (2, 64)), -0.2, 0.2), 0.2, 0.6)
    return dict(in_flight=in_flight, entering=entering, norm_gain=norm_gain, w_gate=w_gate, w_up=w_up, w_down=w_down, routes=routes, combine_weight=combine_weight)


EPSILON = 1e-06

def norm_rows(hidden_rows, norm_gain):
    as_float = hidden_rows.astype(jnp.float32)
    inv_scale = lax.rsqrt(lax.optimization_barrier(jnp.mean(as_float * as_float, axis=-1, keepdims=True)) + EPSILON)
    return (as_float * inv_scale * norm_gain.astype(jnp.float32)).astype(jnp.bfloat16)

def apply_layer(hidden_rows, norm_gain, route_ids, combine, gate_w, up_w, down_w):
    normed = norm_rows(hidden_rows, norm_gain)
    row_total = hidden_rows.shape[0]
    top_count = route_ids.shape[-1]
    flat_routes = route_ids.reshape(-1).astype(jnp.int32)
    flat_weights = combine.reshape(-1)
    most_rows = min(row_total * top_count, 2 * CAP * N_EXPERT)

    def per_expert(running, pieces):
        expert_id, gate_one, up_one, down_one = pieces
        hit_mask = flat_routes == expert_id
        order = jnp.argsort(jnp.where(hit_mask, 0, 1).astype(jnp.int32), stable=True)[:most_rows].astype(jnp.int32)
        chosen = hit_mask[order]
        token_ids = (order // top_count).astype(jnp.int32)
        inputs = normed[token_ids]
        gate_sum = jnp.dot(inputs, gate_one, preferred_element_type=jnp.float32)
        up_sum = jnp.dot(inputs, up_one, preferred_element_type=jnp.float32)
        hidden = (jax.nn.silu(gate_sum) * up_sum).astype(jnp.bfloat16)
        output = jnp.dot(hidden, down_one, preferred_element_type=jnp.float32).astype(jnp.bfloat16)
        scales = jnp.where(chosen, flat_weights[order], jnp.zeros((), flat_weights.dtype))
        scaled = scales[:, None].astype(jnp.float32) * output.astype(jnp.float32)
        return (running.at[token_ids].add(scaled), None)
    start = jnp.zeros((row_total, hidden_rows.shape[1]), jnp.float32)
    expert_ids = jnp.arange(EXPERTS, dtype=jnp.int32)
    summed = lax.scan(per_expert, start, (expert_ids, gate_w, up_w, down_w))[0]
    return (hidden_rows.astype(jnp.float32) + summed).astype(jnp.bfloat16)

def reference(in_flight, entering, norm_gain, w_gate, w_up, w_down, routes, combine_weight):
    carried = [in_flight[section_id] for section_id in range(LAYERS)]
    traced = []
    for tick_index in range(TICKS):
        outputs_now = [apply_layer(carried[section_id], norm_gain[section_id], routes[section_id, tick_index], combine_weight[section_id, tick_index], w_gate[section_id], w_up[section_id], w_down[section_id]) for section_id in range(LAYERS)]
        traced.append(jnp.stack(outputs_now))
        if tick_index + 1 < TICKS:
            carried = [entering[tick_index]] + outputs_now[:-1]
    return jnp.stack(traced)
```

```python
import jax
import jax.numpy as jnp
from jax import lax
from jax.sharding import PartitionSpec as P

TICKS = 2


EPSILON = 1e-06
BLOCK_ROWS = 32
LANE = 128
SUBLANE = 8


def passed_along(x, axis, by):
    devices = lax.axis_size(axis)
    pairs = [(i, i + by) for i in range(devices) if 0 <= i + by < devices]
    return lax.ppermute(x, axis, pairs)


def rms_normed(hidden_rows, norm_gain):
    as_float = hidden_rows.astype(jnp.float32)
    inv_scale = lax.rsqrt(jnp.mean(as_float * as_float, axis=-1, keepdims=True) + EPSILON)
    return (as_float * inv_scale * norm_gain.astype(jnp.float32)).astype(jnp.bfloat16)


def slot_table(route_ids, experts, capacity):
    group_count, row_count, top_count = route_ids.shape
    expert_marks = (route_ids[..., None] == jnp.arange(experts, dtype=jnp.int32)).astype(jnp.int32)
    expert_marks = expert_marks.reshape(group_count, row_count * top_count, experts)
    earlier_marks = jnp.cumsum(expert_marks, axis=1) - expert_marks
    slot_index = jnp.sum(earlier_marks * expert_marks, axis=-1).reshape(
        group_count, row_count, top_count
    )
    group_index = jnp.arange(group_count, dtype=jnp.int32)[:, None, None]
    group_width = group_count * capacity
    positions = route_ids * group_width + group_index * capacity + slot_index
    return positions.reshape(group_count * row_count, top_count)


def wire_shape(rows, width):
    total = rows * width
    if total % (SUBLANE * LANE) == 0:
        return (SUBLANE, total // SUBLANE)
    return (rows, width)


def exchange(chunks):
    experts, rows, width = chunks.shape
    wire = chunks.reshape((experts,) + wire_shape(rows, width))
    moved = lax.all_to_all(wire, "expert", split_axis=0, concat_axis=0, tiled=True)
    return moved.reshape(experts, rows, width)


def apply_layer(hidden_rows, norm_gain, route_ids, combine, gate_w, up_w, down_w, experts):
    normed_rows = rms_normed(hidden_rows, norm_gain)
    row_count, model_width = hidden_rows.shape
    top_count = route_ids.shape[-1]
    block_rows = min(BLOCK_ROWS, row_count)
    group_count = row_count // block_rows
    capacity = max(2, min(block_rows, block_rows * top_count // experts * 3 // 2))
    groups = route_ids.reshape(group_count, block_rows, top_count)
    positions = slot_table(groups, experts, capacity)
    slot_total = experts * group_count * capacity
    flat_slots = positions.reshape(-1)
    pick_table = flat_slots[None, :] == jnp.arange(slot_total, dtype=jnp.int32)[:, None]
    pick_table = jnp.sum(
        pick_table.reshape(slot_total, row_count, top_count).astype(jnp.int32), axis=-1
    ).astype(jnp.bfloat16)
    outgoing = jnp.dot(pick_table, normed_rows, preferred_element_type=jnp.float32).astype(
        jnp.bfloat16
    )
    received = exchange(outgoing.reshape(experts, group_count * capacity, model_width))
    inputs = received.reshape(slot_total, model_width)
    gate_sum = jnp.dot(inputs, gate_w, preferred_element_type=jnp.float32)
    up_sum = jnp.dot(inputs, up_w, preferred_element_type=jnp.float32)
    hidden = (jax.nn.silu(gate_sum) * up_sum).astype(jnp.bfloat16)
    result = jnp.dot(hidden, down_w, preferred_element_type=jnp.float32).astype(jnp.bfloat16)
    returned = exchange(result.reshape(experts, group_count * capacity, model_width))
    returned = returned.reshape(slot_total, model_width)
    residual = hidden_rows.astype(jnp.float32)
    hit_table = (flat_slots[:, None] == jnp.arange(slot_total, dtype=jnp.int32)[None, :]).astype(
        jnp.float32
    )
    mixing = jnp.sum(
        hit_table.reshape(row_count, top_count, slot_total) * combine[:, :, None], axis=1
    )
    mixing_high = mixing.astype(jnp.bfloat16)
    mixing_low = (mixing - mixing_high.astype(jnp.float32)).astype(jnp.bfloat16)
    branch_sum = jnp.dot(mixing_high, returned, preferred_element_type=jnp.float32)
    branch_sum = branch_sum + jnp.dot(mixing_low, returned, preferred_element_type=jnp.float32)
    return (residual + branch_sum).astype(jnp.bfloat16)


def local(in_flight, entering, norm_gain, w_gate, w_up, w_down, routes, combine_weight):
    section_index = lax.axis_index("section")
    experts = lax.axis_size("expert") * w_gate.shape[1]
    carried = in_flight[0]
    traced = []
    for tick_index in range(TICKS):
        layer_out = apply_layer(
            carried,
            norm_gain[0],
            routes[0, tick_index],
            combine_weight[0, tick_index],
            w_gate[0, 0],
            w_up[0, 0],
            w_down[0, 0],
            experts,
        )
        traced.append(layer_out)
        if tick_index + 1 < TICKS:
            shifted = passed_along(layer_out, "section", 1)
            carried = jnp.where(section_index == 0, entering[tick_index], shifted)
    return jnp.stack(traced)[:, None]


def solution(mesh):
    placed = (
        P("section", "expert", None),
        P(None, "expert", None),
        P("section", None),
        P("section", "expert", None, None),
        P("section", "expert", None, None),
        P("section", "expert", None, None),
        P("section", None, "expert", None),
        P("section", None, "expert", None),
    )
    return jax.shard_map(
        local,
        mesh=mesh,
        in_specs=placed,
        out_specs=P(None, "section", "expert", None),
        check_vma=False,
    )
```

```python
import jax
import jax.numpy as jnp
from jax import lax
from jax.sharding import PartitionSpec as P

TICKS = 2


EPSILON = 1e-06
BLOCK_ROWS = 32
SUBLANE = 8


def passed_along(x, axis, by):
    devices = lax.axis_size(axis)
    pairs = [(i, i + by) for i in range(devices) if 0 <= i + by < devices]
    return lax.ppermute(x, axis, pairs)


def rms_normed(hidden_rows, norm_gain):
    as_float = hidden_rows.astype(jnp.float32)
    inv_scale = lax.rsqrt(jnp.mean(as_float * as_float, axis=-1, keepdims=True) + EPSILON)
    return (as_float * inv_scale * norm_gain.astype(jnp.float32)).astype(jnp.bfloat16)


def slot_table(route_ids, experts, capacity):
    group_count, row_count, top_count = route_ids.shape
    expert_marks = (route_ids[..., None] == jnp.arange(experts, dtype=jnp.int32)).astype(jnp.int32)
    expert_marks = expert_marks.reshape(group_count, row_count * top_count, experts)
    earlier_marks = jnp.cumsum(expert_marks, axis=1) - expert_marks
    slot_index = jnp.sum(earlier_marks * expert_marks, axis=-1).reshape(
        group_count, row_count, top_count
    )
    group_index = jnp.arange(group_count, dtype=jnp.int32)[:, None, None]
    group_width = group_count * capacity
    positions = route_ids * group_width + group_index * capacity + slot_index
    return positions.reshape(group_count * row_count, top_count)


def wire_slots(experts, width):
    extra = width - SUBLANE
    pieces = SUBLANE // extra
    row = jnp.arange(SUBLANE, dtype=jnp.int32)
    base = jnp.arange(experts, dtype=jnp.int32)[:, None] * width
    full_slot = (base + row[None, :]).reshape(-1)
    part_slot = (base + SUBLANE + row[None, :] % extra).reshape(-1)
    part_piece = jnp.broadcast_to(row[None, :] // extra, (experts, SUBLANE)).reshape(-1)
    return full_slot, part_slot, part_piece, pieces


def apply_layer(hidden_rows, norm_gain, route_ids, combine, gate_w, up_w, down_w, experts):
    normed_rows = rms_normed(hidden_rows, norm_gain)
    row_count, model_width = hidden_rows.shape
    top_count = route_ids.shape[-1]
    block_rows = min(BLOCK_ROWS, row_count)
    group_count = row_count // block_rows
    capacity = max(2, min(block_rows, block_rows * top_count // experts * 3 // 2))
    width = group_count * capacity
    groups = route_ids.reshape(group_count, block_rows, top_count)
    positions = slot_table(groups, experts, capacity)
    full_slot, part_slot, part_piece, pieces = wire_slots(experts, width)
    piece_width = model_width // pieces
    wire_rows = experts * SUBLANE

    hits_full = positions[:, :, None] == full_slot[None, None, :]
    hits_part = positions[:, :, None] == part_slot[None, None, :]
    pick_full = jnp.sum(hits_full.astype(jnp.int32), axis=1).astype(jnp.bfloat16).T
    pick_part = jnp.sum(hits_part.astype(jnp.int32), axis=1).astype(jnp.bfloat16).T
    send_full = jnp.dot(pick_full, normed_rows, preferred_element_type=jnp.float32)
    send_part = jnp.zeros((wire_rows, piece_width), jnp.float32)
    for piece in range(pieces):
        chosen = (part_piece == piece)[:, None]
        lanes = normed_rows[:, piece * piece_width:(piece + 1) * piece_width]
        send_part = send_part + jnp.dot(
            jnp.where(chosen, pick_part, jnp.zeros_like(pick_part)),
            lanes,
            preferred_element_type=jnp.float32,
        )
    outgoing = jnp.concatenate(
        [
            send_full.astype(jnp.bfloat16).reshape(experts, SUBLANE, model_width),
            send_part.astype(jnp.bfloat16).reshape(experts, SUBLANE, piece_width),
        ],
        axis=-1,
    )
    received = lax.all_to_all(outgoing, "expert", split_axis=0, concat_axis=0, tiled=True)

    extra = width - SUBLANE
    full_rows = received[:, :, :model_width].reshape(wire_rows, model_width)
    part_rows = received[:, :, model_width:].reshape(wire_rows, piece_width)
    joined_row = (
        jnp.arange(experts, dtype=jnp.int32)[:, None] * extra
        + jnp.arange(extra, dtype=jnp.int32)[None, :]
    ).reshape(-1)
    joined_count = experts * extra
    wire_joined = (
        jnp.arange(experts, dtype=jnp.int32)[:, None] * extra
        + jnp.arange(SUBLANE, dtype=jnp.int32)[None, :] % extra
    ).reshape(-1)
    gather_pieces = []
    spread = []
    for piece in range(pieces):
        table = (wire_joined[None, :] == joined_row[:, None]) & (part_piece == piece)[None, :]
        table = table.astype(jnp.bfloat16)
        spread.append(table)
        gather_pieces.append(
            jnp.dot(table, part_rows, preferred_element_type=jnp.float32).astype(jnp.bfloat16)
        )
    joined_rows = jnp.concatenate(gather_pieces, axis=-1)
    inputs = jnp.concatenate([full_rows, joined_rows], axis=0)
    gate_sum = jnp.dot(inputs, gate_w, preferred_element_type=jnp.float32)
    up_sum = jnp.dot(inputs, up_w, preferred_element_type=jnp.float32)
    hidden = (jax.nn.silu(gate_sum) * up_sum).astype(jnp.bfloat16)
    result = jnp.dot(hidden, down_w, preferred_element_type=jnp.float32).astype(jnp.bfloat16)
    result_full = result[:wire_rows]
    result_joined = result[wire_rows:]
    back_part = jnp.zeros((wire_rows, piece_width), jnp.float32)
    for piece in range(pieces):
        back_part = back_part + jnp.dot(
            spread[piece].T,
            result_joined[:, piece * piece_width:(piece + 1) * piece_width],
            preferred_element_type=jnp.float32,
        )
    back = jnp.concatenate(
        [
            result_full.reshape(experts, SUBLANE, model_width),
            back_part.astype(jnp.bfloat16).reshape(experts, SUBLANE, piece_width),
        ],
        axis=-1,
    )
    returned = lax.all_to_all(back, "expert", split_axis=0, concat_axis=0, tiled=True)
    back_full = returned[:, :, :model_width].reshape(wire_rows, model_width)
    back_rows = returned[:, :, model_width:].reshape(wire_rows, piece_width)

    weights = combine[:, :, None]
    mix_full = jnp.sum(jnp.where(hits_full, weights, 0.0), axis=1)
    mix_part = jnp.sum(jnp.where(hits_part, weights, 0.0), axis=1)

    def mixed(mix, rows):
        high = mix.astype(jnp.bfloat16)
        low = (mix - high.astype(jnp.float32)).astype(jnp.bfloat16)
        total = jnp.dot(high, rows, preferred_element_type=jnp.float32)
        return total + jnp.dot(low, rows, preferred_element_type=jnp.float32)

    branch_full = mixed(mix_full, back_full)
    branch_part = [
        mixed(jnp.where((part_piece == piece)[None, :], mix_part, 0.0), back_rows)
        for piece in range(pieces)
    ]
    branch_sum = branch_full + jnp.concatenate(branch_part, axis=-1)
    residual = hidden_rows.astype(jnp.float32)
    return (residual + branch_sum).astype(jnp.bfloat16)


def local(in_flight, entering, norm_gain, w_gate, w_up, w_down, routes, combine_weight):
    section_index = lax.axis_index("section")
    experts = lax.axis_size("expert") * w_gate.shape[1]
    carried = in_flight[0]
    traced = []
    for tick_index in range(TICKS):
        layer_out = apply_layer(
            carried,
            norm_gain[0],
            routes[0, tick_index],
            combine_weight[0, tick_index],
            w_gate[0, 0],
            w_up[0, 0],
            w_down[0, 0],
            experts,
        )
        traced.append(layer_out)
        if tick_index + 1 < TICKS:
            shifted = passed_along(layer_out, "section", 1)
            carried = jnp.where(section_index == 0, entering[tick_index], shifted)
    return jnp.stack(traced)[:, None]


def solution(mesh):
    placed = (
        P("section", "expert", None),
        P(None, "expert", None),
        P("section", None),
        P("section", "expert", None, None),
        P("section", "expert", None, None),
        P("section", "expert", None, None),
        P("section", None, "expert", None),
        P("section", None, "expert", None),
    )
    return jax.shard_map(
        local,
        mesh=mesh,
        in_specs=placed,
        out_specs=P(None, "section", "expert", None),
        check_vma=False,
    )
```

```python
import jax
import jax.numpy as jnp
from jax import lax
from jax.sharding import PartitionSpec as P

TICKS = 2


EPSILON = 1e-06
BLOCK_ROWS = 32
SUBLANE = 8


def passed_along(x, axis, by):
    devices = lax.axis_size(axis)
    pairs = [(i, i + by) for i in range(devices) if 0 <= i + by < devices]
    return lax.ppermute(x, axis, pairs)


def rms_normed(hidden_rows, norm_gain):
    as_float = hidden_rows.astype(jnp.float32)
    inv_scale = lax.rsqrt(jnp.mean(as_float * as_float, axis=-1, keepdims=True) + EPSILON)
    return (as_float * inv_scale * norm_gain.astype(jnp.float32)).astype(jnp.bfloat16)


def slot_table(route_ids, experts, capacity):
    group_count, row_count, top_count = route_ids.shape
    expert_marks = (route_ids[..., None] == jnp.arange(experts, dtype=jnp.int32)).astype(jnp.int32)
    expert_marks = expert_marks.reshape(group_count, row_count * top_count, experts)
    earlier_marks = jnp.cumsum(expert_marks, axis=1) - expert_marks
    slot_index = jnp.sum(earlier_marks * expert_marks, axis=-1).reshape(
        group_count, row_count, top_count
    )
    group_index = jnp.arange(group_count, dtype=jnp.int32)[:, None, None]
    group_width = group_count * capacity
    positions = route_ids * group_width + group_index * capacity + slot_index
    return positions.reshape(group_count * row_count, top_count)


def wire_slots(experts, width):
    extra = width - SUBLANE
    pieces = SUBLANE // extra
    row = jnp.arange(SUBLANE, dtype=jnp.int32)
    base = jnp.arange(experts, dtype=jnp.int32)[:, None] * width
    full_slot = (base + row[None, :]).reshape(-1)
    part_slot = (base + SUBLANE + row[None, :] % extra).reshape(-1)
    part_piece = jnp.broadcast_to(row[None, :] // extra, (experts, SUBLANE)).reshape(-1)
    return full_slot, part_slot, part_piece, pieces


def apply_layer(hidden_rows, norm_gain, route_ids, combine, gate_w, up_w, down_w, experts):
    normed_rows = rms_normed(hidden_rows, norm_gain)
    row_count, model_width = hidden_rows.shape
    top_count = route_ids.shape[-1]
    block_rows = min(BLOCK_ROWS, row_count)
    group_count = row_count // block_rows
    capacity = max(2, min(block_rows, block_rows * top_count // experts * 3 // 2))
    width = group_count * capacity
    groups = route_ids.reshape(group_count, block_rows, top_count)
    positions = slot_table(groups, experts, capacity)
    full_slot, part_slot, part_piece, pieces = wire_slots(experts, width)
    piece_width = model_width // pieces
    wire_rows = experts * SUBLANE

    hits_full = positions[:, :, None] == full_slot[None, None, :]
    hits_part = positions[:, :, None] == part_slot[None, None, :]
    pick_full = jnp.sum(hits_full.astype(jnp.int32), axis=1).astype(jnp.bfloat16).T
    pick_part = jnp.sum(hits_part.astype(jnp.int32), axis=1).astype(jnp.bfloat16).T
    send_full = jnp.dot(pick_full, normed_rows, preferred_element_type=jnp.float32)
    send_part = jnp.zeros((wire_rows, piece_width), jnp.float32)
    for piece in range(pieces):
        chosen = (part_piece == piece)[:, None]
        lanes = normed_rows[:, piece * piece_width:(piece + 1) * piece_width]
        send_part = send_part + jnp.dot(
            jnp.where(chosen, pick_part, jnp.zeros_like(pick_part)),
            lanes,
            preferred_element_type=jnp.float32,
        )
    outgoing = jnp.concatenate(
        [
            send_full.astype(jnp.bfloat16).reshape(experts, SUBLANE, model_width),
            send_part.astype(jnp.bfloat16).reshape(experts, SUBLANE, piece_width),
        ],
        axis=-1,
    )
    received = lax.all_to_all(outgoing, "expert", split_axis=0, concat_axis=0, tiled=True)

    extra = width - SUBLANE
    full_rows = received[:, :, :model_width].reshape(wire_rows, model_width)
    part_rows = received[:, :, model_width:].reshape(wire_rows, piece_width)
    joined_row = (
        jnp.arange(experts, dtype=jnp.int32)[:, None] * extra
        + jnp.arange(extra, dtype=jnp.int32)[None, :]
    ).reshape(-1)
    joined_count = experts * extra
    wire_joined = (
        jnp.arange(experts, dtype=jnp.int32)[:, None] * extra
        + jnp.arange(SUBLANE, dtype=jnp.int32)[None, :] % extra
    ).reshape(-1)
    gather_pieces = []
    spread = []
    for piece in range(pieces):
        table = (wire_joined[None, :] == joined_row[:, None]) & (part_piece == piece)[None, :]
        table = table.astype(jnp.bfloat16)
        spread.append(table)
        gather_pieces.append(
            jnp.dot(table, part_rows, preferred_element_type=jnp.float32).astype(jnp.bfloat16)
        )
    joined_rows = jnp.concatenate(gather_pieces, axis=-1)
    inputs = jnp.concatenate([full_rows, joined_rows], axis=0)
    gate_sum = jnp.dot(inputs, gate_w, preferred_element_type=jnp.float32)
    up_sum = jnp.dot(inputs, up_w, preferred_element_type=jnp.float32)
    hidden = (jax.nn.silu(gate_sum) * up_sum).astype(jnp.bfloat16)
    hidden = lax.optimization_barrier(hidden)
    result = jnp.dot(hidden, down_w, preferred_element_type=jnp.float32).astype(jnp.bfloat16)
    result_full = result[:wire_rows]
    result_joined = result[wire_rows:]
    back_part = jnp.zeros((wire_rows, piece_width), jnp.float32)
    for piece in range(pieces):
        back_part = back_part + jnp.dot(
            spread[piece].T,
            result_joined[:, piece * piece_width:(piece + 1) * piece_width],
            preferred_element_type=jnp.float32,
        )
    back = jnp.concatenate(
        [
            result_full.reshape(experts, SUBLANE, model_width),
            back_part.astype(jnp.bfloat16).reshape(experts, SUBLANE, piece_width),
        ],
        axis=-1,
    )
    returned = lax.all_to_all(back, "expert", split_axis=0, concat_axis=0, tiled=True)
    back_full = returned[:, :, :model_width].reshape(wire_rows, model_width)
    back_rows = returned[:, :, model_width:].reshape(wire_rows, piece_width)

    weights = combine[:, :, None]
    mix_full = jnp.sum(jnp.where(hits_full, weights, 0.0), axis=1)
    mix_part = jnp.sum(jnp.where(hits_part, weights, 0.0), axis=1)

    def split(mix):
        high = mix.astype(jnp.bfloat16)
        low = (mix - high.astype(jnp.float32)).astype(jnp.bfloat16)
        return [high, low]

    full_parts = split(mix_full)
    full_sum = jnp.dot(
        jnp.concatenate(full_parts, axis=0), back_full, preferred_element_type=jnp.float32
    )
    branch_full = full_sum[:row_count] + full_sum[row_count:]
    part_parts = []
    for piece in range(pieces):
        part_parts += split(jnp.where((part_piece == piece)[None, :], mix_part, 0.0))
    part_sum = jnp.dot(
        jnp.concatenate(part_parts, axis=0), back_rows, preferred_element_type=jnp.float32
    )
    branch_part = [
        part_sum[(2 * piece) * row_count:(2 * piece + 1) * row_count]
        + part_sum[(2 * piece + 1) * row_count:(2 * piece + 2) * row_count]
        for piece in range(pieces)
    ]
    branch_sum = branch_full + jnp.concatenate(branch_part, axis=-1)
    residual = hidden_rows.astype(jnp.float32)
    return (residual + branch_sum).astype(jnp.bfloat16)


def local(in_flight, entering, norm_gain, w_gate, w_up, w_down, routes, combine_weight):
    section_index = lax.axis_index("section")
    experts = lax.axis_size("expert") * w_gate.shape[1]
    carried = in_flight[0]
    traced = []
    for tick_index in range(TICKS):
        layer_out = apply_layer(
            carried,
            norm_gain[0],
            routes[0, tick_index],
            combine_weight[0, tick_index],
            w_gate[0, 0],
            w_up[0, 0],
            w_down[0, 0],
            experts,
        )
        traced.append(layer_out)
        if tick_index + 1 < TICKS:
            shifted = passed_along(layer_out, "section", 1)
            carried = jnp.where(section_index == 0, entering[tick_index], shifted)
    return jnp.stack(traced)[:, None]


def solution(mesh):
    placed = (
        P("section", "expert", None),
        P(None, "expert", None),
        P("section", None),
        P("section", "expert", None, None),
        P("section", "expert", None, None),
        P("section", "expert", None, None),
        P("section", None, "expert", None),
        P("section", None, "expert", None),
    )
    return jax.shard_map(
        local,
        mesh=mesh,
        in_specs=placed,
        out_specs=P(None, "section", "expert", None),
        check_vma=False,
    )
```

```python
import jax
import jax.numpy as jnp
from jax import lax
from jax.sharding import PartitionSpec as P

TICKS = 2


EPSILON = 1e-06
BLOCK_ROWS = 32
SUBLANE = 8


def passed_along(x, axis, by):
    devices = lax.axis_size(axis)
    pairs = [(i, i + by) for i in range(devices) if 0 <= i + by < devices]
    return lax.ppermute(x, axis, pairs)


def rms_normed(hidden_rows, norm_gain):
    as_float = hidden_rows.astype(jnp.float32)
    inv_scale = lax.rsqrt(jnp.mean(as_float * as_float, axis=-1, keepdims=True) + EPSILON)
    return (as_float * inv_scale * norm_gain.astype(jnp.float32)).astype(jnp.bfloat16)


def slot_table(route_ids, experts, capacity):
    group_count, row_count, top_count = route_ids.shape
    flat = row_count * top_count
    expert_marks = (route_ids[..., None] == jnp.arange(experts, dtype=jnp.int32)).astype(jnp.bfloat16)
    expert_marks = expert_marks.reshape(group_count, flat, experts)
    earlier = (
        jnp.arange(flat, dtype=jnp.int32)[:, None] > jnp.arange(flat, dtype=jnp.int32)[None, :]
    ).astype(jnp.bfloat16)
    earlier_marks = jnp.einsum(
        "ij,gje->gie", earlier, expert_marks, preferred_element_type=jnp.float32
    )
    slot_index = jnp.sum(earlier_marks * expert_marks.astype(jnp.float32), axis=-1)
    slot_index = slot_index.astype(jnp.int32).reshape(group_count, row_count, top_count)
    group_index = jnp.arange(group_count, dtype=jnp.int32)[:, None, None]
    group_width = group_count * capacity
    positions = route_ids * group_width + group_index * capacity + slot_index
    return positions.reshape(group_count * row_count, top_count)


def wire_slots(experts, width):
    extra = width - SUBLANE
    pieces = SUBLANE // extra
    row = jnp.arange(SUBLANE, dtype=jnp.int32)
    base = jnp.arange(experts, dtype=jnp.int32)[:, None] * width
    full_slot = (base + row[None, :]).reshape(-1)
    part_slot = (base + SUBLANE + row[None, :] % extra).reshape(-1)
    part_piece = jnp.broadcast_to(row[None, :] // extra, (experts, SUBLANE)).reshape(-1)
    return full_slot, part_slot, part_piece, pieces


def apply_layer(hidden_rows, norm_gain, route_ids, combine, gate_up_w, down_w, experts):
    normed_rows = rms_normed(hidden_rows, norm_gain)
    row_count, model_width = hidden_rows.shape
    top_count = route_ids.shape[-1]
    block_rows = min(BLOCK_ROWS, row_count)
    group_count = row_count // block_rows
    capacity = max(2, min(block_rows, block_rows * top_count // experts * 3 // 2))
    width = group_count * capacity
    groups = route_ids.reshape(group_count, block_rows, top_count)
    positions = slot_table(groups, experts, capacity)
    full_slot, part_slot, part_piece, pieces = wire_slots(experts, width)
    piece_width = model_width // pieces
    wire_rows = experts * SUBLANE

    hits_full = positions[:, :, None] == full_slot[None, None, :]
    hits_part = positions[:, :, None] == part_slot[None, None, :]
    pick_full = jnp.sum(hits_full.astype(jnp.int32), axis=1).astype(jnp.bfloat16).T
    pick_part = jnp.sum(hits_part.astype(jnp.int32), axis=1).astype(jnp.bfloat16).T
    pick_pieces = [
        jnp.where((part_piece == piece)[:, None], pick_part, jnp.zeros_like(pick_part))
        for piece in range(pieces)
    ]
    sources = [jnp.pad(normed_rows, ((0, 0), (0, piece_width)))]
    for piece in range(pieces):
        lanes = normed_rows[:, piece * piece_width:(piece + 1) * piece_width]
        sources.append(jnp.pad(lanes, ((0, 0), (model_width, 0))))
    outgoing = jnp.dot(
        jnp.concatenate([pick_full] + pick_pieces, axis=1),
        jnp.concatenate(sources, axis=0),
        preferred_element_type=jnp.float32,
    ).astype(jnp.bfloat16)
    outgoing = outgoing.reshape(experts, SUBLANE, model_width + piece_width)
    received = lax.all_to_all(outgoing, "expert", split_axis=0, concat_axis=0, tiled=True)

    extra = width - SUBLANE
    full_rows = received[:, :, :model_width].reshape(wire_rows, model_width)
    part_rows = received[:, :, model_width:].reshape(wire_rows, piece_width)
    joined_row = (
        jnp.arange(experts, dtype=jnp.int32)[:, None] * extra
        + jnp.arange(extra, dtype=jnp.int32)[None, :]
    ).reshape(-1)
    joined_count = experts * extra
    wire_joined = (
        jnp.arange(experts, dtype=jnp.int32)[:, None] * extra
        + jnp.arange(SUBLANE, dtype=jnp.int32)[None, :] % extra
    ).reshape(-1)
    gather_pieces = []
    spread = []
    for piece in range(pieces):
        table = (wire_joined[None, :] == joined_row[:, None]) & (part_piece == piece)[None, :]
        table = table.astype(jnp.bfloat16)
        spread.append(table)
        gather_pieces.append(
            jnp.dot(table, part_rows, preferred_element_type=jnp.float32).astype(jnp.bfloat16)
        )
    joined_rows = jnp.concatenate(gather_pieces, axis=-1)
    inputs = jnp.concatenate([full_rows, joined_rows], axis=0)
    gate_up = jnp.dot(inputs, gate_up_w, preferred_element_type=jnp.float32)
    ff = gate_up.shape[-1] // 2
    gate_sum, up_sum = gate_up[:, :ff], gate_up[:, ff:]
    hidden = (jax.nn.silu(gate_sum) * up_sum).astype(jnp.bfloat16)
    hidden = lax.optimization_barrier(hidden)
    result = jnp.dot(hidden, down_w, preferred_element_type=jnp.float32).astype(jnp.bfloat16)
    result_full = result[:wire_rows]
    result_joined = result[wire_rows:]
    back_part = jnp.zeros((wire_rows, piece_width), jnp.float32)
    for piece in range(pieces):
        back_part = back_part + jnp.dot(
            spread[piece].T,
            result_joined[:, piece * piece_width:(piece + 1) * piece_width],
            preferred_element_type=jnp.float32,
        )
    back = jnp.concatenate(
        [
            result_full.reshape(experts, SUBLANE, model_width),
            back_part.astype(jnp.bfloat16).reshape(experts, SUBLANE, piece_width),
        ],
        axis=-1,
    )
    returned = lax.all_to_all(back, "expert", split_axis=0, concat_axis=0, tiled=True)
    back_full = returned[:, :, :model_width].reshape(wire_rows, model_width)
    back_rows = returned[:, :, model_width:].reshape(wire_rows, piece_width)

    weights = combine[:, :, None]
    mix_full = jnp.sum(jnp.where(hits_full, weights, 0.0), axis=1)
    mix_part = jnp.sum(jnp.where(hits_part, weights, 0.0), axis=1)

    def split(mix):
        high = mix.astype(jnp.bfloat16)
        low = (mix - high.astype(jnp.float32)).astype(jnp.bfloat16)
        return [high, low]

    full_parts = split(mix_full)
    full_sum = jnp.dot(
        jnp.concatenate(full_parts, axis=0), back_full, preferred_element_type=jnp.float32
    )
    branch_full = full_sum[:row_count] + full_sum[row_count:]
    part_parts = []
    for piece in range(pieces):
        part_parts += split(jnp.where((part_piece == piece)[None, :], mix_part, 0.0))
    part_sum = jnp.dot(
        jnp.concatenate(part_parts, axis=0), back_rows, preferred_element_type=jnp.float32
    )
    branch_part = [
        part_sum[(2 * piece) * row_count:(2 * piece + 1) * row_count]
        + part_sum[(2 * piece + 1) * row_count:(2 * piece + 2) * row_count]
        for piece in range(pieces)
    ]
    branch_sum = branch_full + jnp.concatenate(branch_part, axis=-1)
    residual = hidden_rows.astype(jnp.float32)
    return (residual + branch_sum).astype(jnp.bfloat16)


def local(in_flight, entering, norm_gain, w_gate, w_up, w_down, routes, combine_weight):
    section_index = lax.axis_index("section")
    experts = lax.axis_size("expert") * w_gate.shape[1]
    carried = in_flight[0]
    gate_up_w = jnp.concatenate([w_gate[0, 0], w_up[0, 0]], axis=-1)
    traced = []
    for tick_index in range(TICKS):
        layer_out = apply_layer(
            carried,
            norm_gain[0],
            routes[0, tick_index],
            combine_weight[0, tick_index],
            gate_up_w,
            w_down[0, 0],
            experts,
        )
        traced.append(layer_out)
        if tick_index + 1 < TICKS:
            shifted = passed_along(layer_out, "section", 1)
            carried = jnp.where(section_index == 0, entering[tick_index], shifted)
    return jnp.stack(traced)[:, None]


def solution(mesh):
    placed = (
        P("section", "expert", None),
        P(None, "expert", None),
        P("section", None),
        P("section", "expert", None, None),
        P("section", "expert", None, None),
        P("section", "expert", None, None),
        P("section", None, "expert", None),
        P("section", None, "expert", None),
    )
    return jax.shard_map(
        local,
        mesh=mesh,
        in_specs=placed,
        out_specs=P(None, "section", "expert", None),
        check_vma=False,
    )
```

```python
import jax
import jax.numpy as jnp
from jax import lax
from jax.sharding import PartitionSpec as P

TICKS = 2


EPSILON = 1e-06
BLOCK_ROWS = 32
SUBLANE = 8


def passed_along(x, axis, by):
    devices = lax.axis_size(axis)
    pairs = [(i, i + by) for i in range(devices) if 0 <= i + by < devices]
    return lax.ppermute(x, axis, pairs)


def rms_normed(hidden_rows, norm_gain):
    as_float = hidden_rows.astype(jnp.float32)
    inv_scale = lax.rsqrt(jnp.mean(as_float * as_float, axis=-1, keepdims=True) + EPSILON)
    return (as_float * inv_scale * norm_gain.astype(jnp.float32)).astype(jnp.bfloat16)


def slot_table(route_ids, experts, capacity):
    group_count, row_count, top_count = route_ids.shape
    expert_marks = (route_ids[..., None] == jnp.arange(experts, dtype=jnp.int32)).astype(jnp.int32)
    expert_marks = expert_marks.reshape(group_count, row_count * top_count, experts)
    earlier_marks = jnp.cumsum(expert_marks, axis=1) - expert_marks
    slot_index = jnp.sum(earlier_marks * expert_marks, axis=-1).reshape(
        group_count, row_count, top_count
    )
    group_index = jnp.arange(group_count, dtype=jnp.int32)[:, None, None]
    group_width = group_count * capacity
    positions = route_ids * group_width + group_index * capacity + slot_index
    return positions.reshape(group_count * row_count, top_count)


def wire_slots(experts, width):
    extra = width - SUBLANE
    pieces = SUBLANE // extra
    row = jnp.arange(SUBLANE, dtype=jnp.int32)
    base = jnp.arange(experts, dtype=jnp.int32)[:, None] * width
    full_slot = (base + row[None, :]).reshape(-1)
    part_slot = (base + SUBLANE + row[None, :] % extra).reshape(-1)
    part_piece = jnp.broadcast_to(row[None, :] // extra, (experts, SUBLANE)).reshape(-1)
    return full_slot, part_slot, part_piece, pieces


def apply_layer(hidden_rows, norm_gain, route_ids, combine, gate_up_w, down_w, experts):
    normed_rows = rms_normed(hidden_rows, norm_gain)
    row_count, model_width = hidden_rows.shape
    top_count = route_ids.shape[-1]
    block_rows = min(BLOCK_ROWS, row_count)
    group_count = row_count // block_rows
    capacity = max(2, min(block_rows, block_rows * top_count // experts * 3 // 2))
    width = group_count * capacity
    groups = route_ids.reshape(group_count, block_rows, top_count)
    positions = slot_table(groups, experts, capacity)
    full_slot, part_slot, part_piece, pieces = wire_slots(experts, width)
    piece_width = model_width // pieces
    wire_rows = experts * SUBLANE

    hits_full = positions[:, :, None] == full_slot[None, None, :]
    hits_part = positions[:, :, None] == part_slot[None, None, :]
    pick_full = jnp.sum(hits_full.astype(jnp.int32), axis=1).astype(jnp.bfloat16).T
    pick_part = jnp.sum(hits_part.astype(jnp.int32), axis=1).astype(jnp.bfloat16).T
    send_full = jnp.dot(pick_full, normed_rows, preferred_element_type=jnp.float32)
    send_part = jnp.zeros((wire_rows, piece_width), jnp.float32)
    for piece in range(pieces):
        chosen = (part_piece == piece)[:, None]
        lanes = normed_rows[:, piece * piece_width:(piece + 1) * piece_width]
        send_part = send_part + jnp.dot(
            jnp.where(chosen, pick_part, jnp.zeros_like(pick_part)),
            lanes,
            preferred_element_type=jnp.float32,
        )
    outgoing = jnp.concatenate(
        [
            send_full.astype(jnp.bfloat16).reshape(experts, SUBLANE, model_width),
            send_part.astype(jnp.bfloat16).reshape(experts, SUBLANE, piece_width),
        ],
        axis=-1,
    )
    received = lax.all_to_all(outgoing, "expert", split_axis=0, concat_axis=0, tiled=True)

    extra = width - SUBLANE
    full_rows = received[:, :, :model_width].reshape(wire_rows, model_width)
    part_rows = received[:, :, model_width:].reshape(wire_rows, piece_width)
    joined_row = (
        jnp.arange(experts, dtype=jnp.int32)[:, None] * extra
        + jnp.arange(extra, dtype=jnp.int32)[None, :]
    ).reshape(-1)
    joined_count = experts * extra
    wire_joined = (
        jnp.arange(experts, dtype=jnp.int32)[:, None] * extra
        + jnp.arange(SUBLANE, dtype=jnp.int32)[None, :] % extra
    ).reshape(-1)
    gather_pieces = []
    spread = []
    for piece in range(pieces):
        table = (wire_joined[None, :] == joined_row[:, None]) & (part_piece == piece)[None, :]
        table = table.astype(jnp.bfloat16)
        spread.append(table)
        gather_pieces.append(
            jnp.dot(table, part_rows, preferred_element_type=jnp.float32).astype(jnp.bfloat16)
        )
    joined_rows = jnp.concatenate(gather_pieces, axis=-1)
    inputs = jnp.concatenate([full_rows, joined_rows], axis=0)
    gate_up = jnp.dot(inputs, gate_up_w, preferred_element_type=jnp.float32)
    ff = gate_up.shape[-1] // 2
    gate_sum, up_sum = gate_up[:, :ff], gate_up[:, ff:]
    hidden = (jax.nn.silu(gate_sum) * up_sum).astype(jnp.bfloat16)
    hidden = lax.optimization_barrier(hidden)
    result = jnp.dot(hidden, down_w, preferred_element_type=jnp.float32).astype(jnp.bfloat16)
    result_full = result[:wire_rows]
    result_joined = result[wire_rows:]
    back_part = jnp.zeros((wire_rows, piece_width), jnp.float32)
    for piece in range(pieces):
        back_part = back_part + jnp.dot(
            spread[piece].T,
            result_joined[:, piece * piece_width:(piece + 1) * piece_width],
            preferred_element_type=jnp.float32,
        )
    back = jnp.concatenate(
        [
            result_full.reshape(experts, SUBLANE, model_width),
            back_part.astype(jnp.bfloat16).reshape(experts, SUBLANE, piece_width),
        ],
        axis=-1,
    )
    returned = lax.all_to_all(back, "expert", split_axis=0, concat_axis=0, tiled=True)
    back_full = returned[:, :, :model_width].reshape(wire_rows, model_width)
    back_rows = returned[:, :, model_width:].reshape(wire_rows, piece_width)

    weights = combine[:, :, None]
    mix_full = jnp.sum(jnp.where(hits_full, weights, 0.0), axis=1)
    mix_part = jnp.sum(jnp.where(hits_part, weights, 0.0), axis=1)

    def split(mix):
        high = mix.astype(jnp.bfloat16)
        low = (mix - high.astype(jnp.float32)).astype(jnp.bfloat16)
        return [high, low]

    full_parts = split(mix_full)
    full_sum = jnp.dot(
        jnp.concatenate(full_parts, axis=0), back_full, preferred_element_type=jnp.float32
    )
    branch_full = full_sum[:row_count] + full_sum[row_count:]
    part_parts = []
    for piece in range(pieces):
        part_parts += split(jnp.where((part_piece == piece)[None, :], mix_part, 0.0))
    part_sum = jnp.dot(
        jnp.concatenate(part_parts, axis=0), back_rows, preferred_element_type=jnp.float32
    )
    branch_part = [
        part_sum[(2 * piece) * row_count:(2 * piece + 1) * row_count]
        + part_sum[(2 * piece + 1) * row_count:(2 * piece + 2) * row_count]
        for piece in range(pieces)
    ]
    branch_sum = branch_full + jnp.concatenate(branch_part, axis=-1)
    residual = hidden_rows.astype(jnp.float32)
    return (residual + branch_sum).astype(jnp.bfloat16)


def local(in_flight, entering, norm_gain, w_gate, w_up, w_down, routes, combine_weight):
    section_index = lax.axis_index("section")
    experts = lax.axis_size("expert") * w_gate.shape[1]
    carried = in_flight[0]
    gate_up_w = jnp.concatenate([w_gate[0, 0], w_up[0, 0]], axis=-1)
    traced = []
    for tick_index in range(TICKS):
        layer_out = apply_layer(
            carried,
            norm_gain[0],
            routes[0, tick_index],
            combine_weight[0, tick_index],
            gate_up_w,
            w_down[0, 0],
            experts,
        )
        traced.append(layer_out)
        if tick_index + 1 < TICKS:
            shifted = passed_along(layer_out, "section", 1)
            carried = jnp.where(section_index == 0, entering[tick_index], shifted)
    return jnp.stack(traced)[:, None]


def solution(mesh):
    placed = (
        P("section", "expert", None),
        P(None, "expert", None),
        P("section", None),
        P("section", "expert", None, None),
        P("section", "expert", None, None),
        P("section", "expert", None, None),
        P("section", None, "expert", None),
        P("section", None, "expert", None),
    )
    return jax.shard_map(
        local,
        mesh=mesh,
        in_specs=placed,
        out_specs=P(None, "section", "expert", None),
        check_vma=False,
    )
```

```python
import jax
import jax.numpy as jnp
import numpy as np
from jax import lax
from jax.sharding import PartitionSpec as P

TICKS = 2


EPSILON = 1e-06
BLOCK_ROWS = 32
SUBLANE = 8


def passed_along(x, axis, by):
    devices = lax.axis_size(axis)
    pairs = [(i, i + by) for i in range(devices) if 0 <= i + by < devices]
    return lax.ppermute(x, axis, pairs)


def rms_normed(hidden_rows, norm_gain):
    as_float = hidden_rows.astype(jnp.float32)
    inv_scale = lax.rsqrt(jnp.mean(as_float * as_float, axis=-1, keepdims=True) + EPSILON)
    return (as_float * inv_scale * norm_gain.astype(jnp.float32)).astype(jnp.bfloat16)


def slot_table(route_ids, experts, capacity):
    group_count, row_count, top_count = route_ids.shape
    expert_marks = (route_ids[..., None] == jnp.arange(experts, dtype=jnp.int32)).astype(jnp.int32)
    expert_marks = expert_marks.reshape(group_count, row_count * top_count, experts)
    earlier_marks = jnp.cumsum(expert_marks, axis=1) - expert_marks
    slot_index = jnp.sum(earlier_marks * expert_marks, axis=-1).reshape(
        group_count, row_count, top_count
    )
    group_index = jnp.arange(group_count, dtype=jnp.int32)[:, None, None]
    group_width = group_count * capacity
    positions = route_ids * group_width + group_index * capacity + slot_index
    return positions.reshape(group_count * row_count, top_count)


def wire_slots(experts, width):
    extra = width - SUBLANE
    pieces = SUBLANE // extra
    row = np.arange(SUBLANE, dtype=np.int32)
    base = np.arange(experts, dtype=np.int32)[:, None] * width
    full_slot = (base + row[None, :]).reshape(-1)
    part_slot = (base + SUBLANE + row[None, :] % extra).reshape(-1)
    part_piece = np.broadcast_to(row[None, :] // extra, (experts, SUBLANE)).reshape(-1)
    return full_slot, part_slot, part_piece, pieces


def plan(route_ids, combine, experts):
    row_count, top_count = route_ids.shape
    block_rows = min(BLOCK_ROWS, row_count)
    group_count = row_count // block_rows
    capacity = max(2, min(block_rows, block_rows * top_count // experts * 3 // 2))
    width = group_count * capacity
    groups = route_ids.reshape(group_count, block_rows, top_count)
    positions = slot_table(groups, experts, capacity)
    full_slot, part_slot, part_piece, pieces = wire_slots(experts, width)
    hits_full = positions[:, :, None] == full_slot[None, None, :]
    hits_part = positions[:, :, None] == part_slot[None, None, :]
    pick_full = jnp.sum(hits_full.astype(jnp.int32), axis=1).astype(jnp.bfloat16).T
    pick_part = jnp.sum(hits_part.astype(jnp.int32), axis=1).astype(jnp.bfloat16).T
    pick_pieces = [
        jnp.where((part_piece == piece)[:, None], pick_part, jnp.zeros_like(pick_part))
        for piece in range(pieces)
    ]
    weights = combine[:, :, None]
    mix_full = jnp.sum(jnp.where(hits_full, weights, 0.0), axis=1)
    mix_part = jnp.sum(jnp.where(hits_part, weights, 0.0), axis=1)

    def split(mix):
        high = mix.astype(jnp.bfloat16)
        low = (mix - high.astype(jnp.float32)).astype(jnp.bfloat16)
        return [high, low]

    full_lhs = jnp.concatenate(split(mix_full), axis=0)
    part_parts = []
    for piece in range(pieces):
        part_parts += split(jnp.where((part_piece == piece)[None, :], mix_part, 0.0))
    part_lhs = jnp.concatenate(part_parts, axis=0)
    return (pick_full, pick_pieces, full_lhs, part_lhs)


def apply_layer(hidden_rows, norm_gain, tables, gate_up_w, down_w, experts, width, tie=None):
    pick_full, pick_pieces, full_lhs, part_lhs = tables
    extra = width - SUBLANE
    wire_joined = np.asarray(
        np.arange(experts)[:, None] * extra + np.arange(SUBLANE)[None, :] % extra, np.int32
    ).reshape(-1)
    joined_row = np.arange(experts * extra, dtype=np.int32)
    normed_rows = rms_normed(hidden_rows, norm_gain)
    row_count, model_width = hidden_rows.shape
    full_slot, part_slot, part_piece, pieces = wire_slots(experts, width)
    piece_width = model_width // pieces
    wire_rows = experts * SUBLANE

    send_full = jnp.dot(pick_full, normed_rows, preferred_element_type=jnp.float32)
    send_part = jnp.zeros((wire_rows, piece_width), jnp.float32)
    for piece in range(pieces):
        lanes = normed_rows[:, piece * piece_width:(piece + 1) * piece_width]
        send_part = send_part + jnp.dot(
            pick_pieces[piece], lanes, preferred_element_type=jnp.float32
        )
    outgoing = jnp.concatenate(
        [
            send_full.astype(jnp.bfloat16).reshape(experts, SUBLANE, model_width),
            send_part.astype(jnp.bfloat16).reshape(experts, SUBLANE, piece_width),
        ],
        axis=-1,
    )
    if tie is not None:
        outgoing, full_lhs, part_lhs, tie = lax.optimization_barrier(
            (outgoing, full_lhs, part_lhs, tie)
        )
    received = lax.all_to_all(outgoing, "expert", split_axis=0, concat_axis=0, tiled=True)

    full_rows = received[:, :, :model_width].reshape(wire_rows, model_width)
    part_rows = received[:, :, model_width:].reshape(wire_rows, piece_width)
    gather_pieces = []
    spread = []
    for piece in range(pieces):
        table = (wire_joined[None, :] == joined_row[:, None]) & (part_piece == piece)[None, :]
        table = jnp.asarray(table, jnp.bfloat16)
        spread.append(table)
        gather_pieces.append(
            jnp.dot(table, part_rows, preferred_element_type=jnp.float32).astype(jnp.bfloat16)
        )
    joined_rows = jnp.concatenate(gather_pieces, axis=-1)
    inputs = jnp.concatenate([full_rows, joined_rows], axis=0)
    gate_up = jnp.dot(inputs, gate_up_w, preferred_element_type=jnp.float32)
    ff = gate_up.shape[-1] // 2
    gate_sum, up_sum = gate_up[:, :ff], gate_up[:, ff:]
    hidden = (jax.nn.silu(gate_sum) * up_sum).astype(jnp.bfloat16)
    hidden = lax.optimization_barrier(hidden)
    result = jnp.dot(hidden, down_w, preferred_element_type=jnp.float32).astype(jnp.bfloat16)
    result_full = result[:wire_rows]
    result_joined = result[wire_rows:]
    back_part = jnp.zeros((wire_rows, piece_width), jnp.float32)
    for piece in range(pieces):
        back_part = back_part + jnp.dot(
            spread[piece].T,
            result_joined[:, piece * piece_width:(piece + 1) * piece_width],
            preferred_element_type=jnp.float32,
        )
    back = jnp.concatenate(
        [
            result_full.reshape(experts, SUBLANE, model_width),
            back_part.astype(jnp.bfloat16).reshape(experts, SUBLANE, piece_width),
        ],
        axis=-1,
    )
    returned = lax.all_to_all(back, "expert", split_axis=0, concat_axis=0, tiled=True)
    back_full = returned[:, :, :model_width].reshape(wire_rows, model_width)
    back_rows = returned[:, :, model_width:].reshape(wire_rows, piece_width)

    full_sum = jnp.dot(full_lhs, back_full, preferred_element_type=jnp.float32)
    branch_full = full_sum[:row_count] + full_sum[row_count:]
    part_sum = jnp.dot(part_lhs, back_rows, preferred_element_type=jnp.float32)
    branch_part = [
        part_sum[(2 * piece) * row_count:(2 * piece + 1) * row_count]
        + part_sum[(2 * piece + 1) * row_count:(2 * piece + 2) * row_count]
        for piece in range(pieces)
    ]
    branch_sum = branch_full + jnp.concatenate(branch_part, axis=-1)
    residual = hidden_rows.astype(jnp.float32)
    return (residual + branch_sum).astype(jnp.bfloat16), tie


def local(in_flight, entering, norm_gain, w_gate, w_up, w_down, routes, combine_weight):
    section_index = lax.axis_index("section")
    experts = lax.axis_size("expert") * w_gate.shape[1]
    row_count, top_count = routes.shape[2], routes.shape[3]
    block_rows = min(BLOCK_ROWS, row_count)
    capacity = max(2, min(block_rows, block_rows * top_count // experts * 3 // 2))
    width = row_count // block_rows * capacity
    plans = [
        plan(routes[0, tick_index], combine_weight[0, tick_index], experts)
        for tick_index in range(TICKS)
    ]
    carried = in_flight[0]
    gate_up_w = jnp.concatenate([w_gate[0, 0], w_up[0, 0]], axis=-1)
    traced = []
    tie = plans
    for tick_index in range(TICKS):
        layer_out, tie = apply_layer(
            carried,
            norm_gain[0],
            plans[tick_index] if tick_index else tie[0],
            gate_up_w,
            w_down[0, 0],
            experts,
            width,
            tie if tick_index == 0 else None,
        )
        if tick_index == 0:
            plans = tie
        traced.append(layer_out)
        if tick_index + 1 < TICKS:
            shifted = passed_along(layer_out, "section", 1)
            carried = jnp.where(section_index == 0, entering[tick_index], shifted)
    return jnp.stack(traced)[:, None]


def solution(mesh):
    placed = (
        P("section", "expert", None),
        P(None, "expert", None),
        P("section", None),
        P("section", "expert", None, None),
        P("section", "expert", None, None),
        P("section", "expert", None, None),
        P("section", None, "expert", None),
        P("section", None, "expert", None),
    )
    return jax.shard_map(
        local,
        mesh=mesh,
        in_specs=placed,
        out_specs=P(None, "section", "expert", None),
        check_vma=False,
    )
```

```python
import jax
import jax.numpy as jnp
import numpy as np
from jax import lax
from jax.sharding import PartitionSpec as P

TICKS = 2


EPSILON = 1e-06
BLOCK_ROWS = 32
SUBLANE = 8


def passed_along(x, axis, by):
    devices = lax.axis_size(axis)
    pairs = [(i, i + by) for i in range(devices) if 0 <= i + by < devices]
    return lax.ppermute(x, axis, pairs)


def rms_normed(hidden_rows, norm_gain):
    as_float = hidden_rows.astype(jnp.float32)
    inv_scale = lax.rsqrt(jnp.mean(as_float * as_float, axis=-1, keepdims=True) + EPSILON)
    return (as_float * inv_scale * norm_gain.astype(jnp.float32)).astype(jnp.bfloat16)


def slot_table(route_ids, experts, capacity):
    group_count, row_count, top_count = route_ids.shape
    expert_marks = (route_ids[..., None] == jnp.arange(experts, dtype=jnp.int32)).astype(jnp.int32)
    expert_marks = expert_marks.reshape(group_count, row_count * top_count, experts)
    earlier_marks = jnp.cumsum(expert_marks, axis=1) - expert_marks
    slot_index = jnp.sum(earlier_marks * expert_marks, axis=-1).reshape(
        group_count, row_count, top_count
    )
    group_index = jnp.arange(group_count, dtype=jnp.int32)[:, None, None]
    group_width = group_count * capacity
    positions = route_ids * group_width + group_index * capacity + slot_index
    return positions.reshape(group_count * row_count, top_count)


def wire_slots(experts, width):
    extra = width - SUBLANE
    pieces = SUBLANE // extra
    row = np.arange(SUBLANE, dtype=np.int32)
    base = np.arange(experts, dtype=np.int32)[:, None] * width
    full_slot = (base + row[None, :]).reshape(-1)
    part_slot = (base + SUBLANE + row[None, :] % extra).reshape(-1)
    part_piece = np.broadcast_to(row[None, :] // extra, (experts, SUBLANE)).reshape(-1)
    return full_slot, part_slot, part_piece, pieces


def apply_layer(hidden_rows, norm_gain, route_ids, combine, gate_up_w, down_w, experts):
    normed_rows = rms_normed(hidden_rows, norm_gain)
    row_count, model_width = hidden_rows.shape
    top_count = route_ids.shape[-1]
    block_rows = min(BLOCK_ROWS, row_count)
    group_count = row_count // block_rows
    capacity = max(2, min(block_rows, block_rows * top_count // experts * 3 // 2))
    width = group_count * capacity
    groups = route_ids.reshape(group_count, block_rows, top_count)
    positions = slot_table(groups, experts, capacity)
    full_slot, part_slot, part_piece, pieces = wire_slots(experts, width)
    piece_width = model_width // pieces
    wire_rows = experts * SUBLANE

    hits_full = positions[:, :, None] == full_slot[None, None, :]
    hits_part = positions[:, :, None] == part_slot[None, None, :]
    pick_full = jnp.sum(hits_full.astype(jnp.int32), axis=1).astype(jnp.bfloat16).T
    pick_part = jnp.sum(hits_part.astype(jnp.int32), axis=1).astype(jnp.bfloat16).T
    send_full = jnp.dot(pick_full, normed_rows, preferred_element_type=jnp.float32)
    send_part = jnp.zeros((wire_rows, piece_width), jnp.float32)
    for piece in range(pieces):
        chosen = (part_piece == piece)[:, None]
        lanes = normed_rows[:, piece * piece_width:(piece + 1) * piece_width]
        send_part = send_part + jnp.dot(
            jnp.where(chosen, pick_part, jnp.zeros_like(pick_part)),
            lanes,
            preferred_element_type=jnp.float32,
        )
    outgoing = jnp.concatenate(
        [
            send_full.astype(jnp.bfloat16).reshape(experts, SUBLANE, model_width),
            send_part.astype(jnp.bfloat16).reshape(experts, SUBLANE, piece_width),
        ],
        axis=-1,
    )
    received = lax.all_to_all(outgoing, "expert", split_axis=0, concat_axis=0, tiled=True)

    extra = width - SUBLANE
    full_rows = received[:, :, :model_width].reshape(wire_rows, model_width)
    part_rows = received[:, :, model_width:].reshape(wire_rows, piece_width)
    joined_row = np.arange(experts * extra, dtype=np.int32)
    wire_joined = np.asarray(
        np.arange(experts)[:, None] * extra + np.arange(SUBLANE)[None, :] % extra, np.int32
    ).reshape(-1)
    gather_pieces = []
    spread = []
    for piece in range(pieces):
        table = (wire_joined[None, :] == joined_row[:, None]) & (part_piece == piece)[None, :]
        table = jnp.asarray(table, jnp.bfloat16)
        spread.append(table)
        gather_pieces.append(
            jnp.dot(table, part_rows, preferred_element_type=jnp.float32).astype(jnp.bfloat16)
        )
    joined_rows = jnp.concatenate(gather_pieces, axis=-1)
    inputs = jnp.concatenate([full_rows, joined_rows], axis=0)
    gate_up = jnp.dot(inputs, gate_up_w, preferred_element_type=jnp.float32)
    ff = gate_up.shape[-1] // 2
    gate_sum, up_sum = gate_up[:, :ff], gate_up[:, ff:]
    hidden = (jax.nn.silu(gate_sum) * up_sum).astype(jnp.bfloat16)
    hidden = lax.optimization_barrier(hidden)
    result = jnp.dot(hidden, down_w, preferred_element_type=jnp.float32).astype(jnp.bfloat16)
    result_full = result[:wire_rows]
    result_joined = result[wire_rows:]
    back_part = jnp.zeros((wire_rows, piece_width), jnp.float32)
    for piece in range(pieces):
        back_part = back_part + jnp.dot(
            spread[piece].T,
            result_joined[:, piece * piece_width:(piece + 1) * piece_width],
            preferred_element_type=jnp.float32,
        )
    back = jnp.concatenate(
        [
            result_full.reshape(experts, SUBLANE, model_width),
            back_part.astype(jnp.bfloat16).reshape(experts, SUBLANE, piece_width),
        ],
        axis=-1,
    )
    returned = lax.all_to_all(back, "expert", split_axis=0, concat_axis=0, tiled=True)
    back_full = returned[:, :, :model_width].reshape(wire_rows, model_width)
    back_rows = returned[:, :, model_width:].reshape(wire_rows, piece_width)

    weights = combine[:, :, None]
    mix_full = jnp.sum(jnp.where(hits_full, weights, 0.0), axis=1)
    mix_part = jnp.sum(jnp.where(hits_part, weights, 0.0), axis=1)

    def split(mix):
        high = mix.astype(jnp.bfloat16)
        low = (mix - high.astype(jnp.float32)).astype(jnp.bfloat16)
        return [high, low]

    full_parts = split(mix_full)
    full_sum = jnp.dot(
        jnp.concatenate(full_parts, axis=0), back_full, preferred_element_type=jnp.float32
    )
    branch_full = full_sum[:row_count] + full_sum[row_count:]
    part_parts = []
    for piece in range(pieces):
        part_parts += split(jnp.where((part_piece == piece)[None, :], mix_part, 0.0))
    part_sum = jnp.dot(
        jnp.concatenate(part_parts, axis=0), back_rows, preferred_element_type=jnp.float32
    )
    branch_part = [
        part_sum[(2 * piece) * row_count:(2 * piece + 1) * row_count]
        + part_sum[(2 * piece + 1) * row_count:(2 * piece + 2) * row_count]
        for piece in range(pieces)
    ]
    branch_sum = branch_full + jnp.concatenate(branch_part, axis=-1)
    residual = hidden_rows.astype(jnp.float32)
    return (residual + branch_sum).astype(jnp.bfloat16)


def local(in_flight, entering, norm_gain, w_gate, w_up, w_down, routes, combine_weight):
    section_index = lax.axis_index("section")
    experts = lax.axis_size("expert") * w_gate.shape[1]
    carried = in_flight[0]
    gate_up_w = jnp.concatenate([w_gate[0, 0], w_up[0, 0]], axis=-1)
    traced = []
    for tick_index in range(TICKS):
        layer_out = apply_layer(
            carried,
            norm_gain[0],
            routes[0, tick_index],
            combine_weight[0, tick_index],
            gate_up_w,
            w_down[0, 0],
            experts,
        )
        traced.append(layer_out)
        if tick_index + 1 < TICKS:
            shifted = passed_along(layer_out, "section", 1)
            carried = jnp.where(section_index == 0, entering[tick_index], shifted)
    return jnp.stack(traced)[:, None]


def solution(mesh):
    placed = (
        P("section", "expert", None),
        P(None, "expert", None),
        P("section", None),
        P("section", "expert", None, None),
        P("section", "expert", None, None),
        P("section", "expert", None, None),
        P("section", None, "expert", None),
        P("section", None, "expert", None),
    )
    return jax.shard_map(
        local,
        mesh=mesh,
        in_specs=placed,
        out_specs=P(None, "section", "expert", None),
        check_vma=False,
    )
```

```python
import jax
import jax.numpy as jnp
from jax import lax
from jax.sharding import PartitionSpec as P

TICKS = 2


EPSILON = 1e-06
BLOCK_ROWS = 32
SUBLANE = 8


def passed_along(x, axis, by):
    devices = lax.axis_size(axis)
    pairs = [(i, i + by) for i in range(devices) if 0 <= i + by < devices]
    return lax.ppermute(x, axis, pairs)


def rms_normed(hidden_rows, norm_gain):
    as_float = hidden_rows.astype(jnp.float32)
    inv_scale = lax.rsqrt(jnp.mean(as_float * as_float, axis=-1, keepdims=True) + EPSILON)
    return (as_float * inv_scale * norm_gain.astype(jnp.float32)).astype(jnp.bfloat16)


def slot_table(route_ids, experts, capacity):
    group_count, row_count, top_count = route_ids.shape
    expert_marks = (route_ids[..., None] == jnp.arange(experts, dtype=jnp.int32)).astype(jnp.int32)
    expert_marks = expert_marks.reshape(group_count, row_count * top_count, experts)
    earlier_marks = jnp.cumsum(expert_marks, axis=1) - expert_marks
    slot_index = jnp.sum(earlier_marks * expert_marks, axis=-1).reshape(
        group_count, row_count, top_count
    )
    group_index = jnp.arange(group_count, dtype=jnp.int32)[:, None, None]
    group_width = group_count * capacity
    positions = route_ids * group_width + group_index * capacity + slot_index
    return positions.reshape(group_count * row_count, top_count)


def wire_slots(experts, width):
    extra = width - SUBLANE
    pieces = SUBLANE // extra
    row = jnp.arange(SUBLANE, dtype=jnp.int32)
    base = jnp.arange(experts, dtype=jnp.int32)[:, None] * width
    full_slot = (base + row[None, :]).reshape(-1)
    part_slot = (base + SUBLANE + row[None, :] % extra).reshape(-1)
    part_piece = jnp.broadcast_to(row[None, :] // extra, (experts, SUBLANE)).reshape(-1)
    return full_slot, part_slot, part_piece, pieces


def apply_layer(hidden_rows, norm_gain, route_ids, combine, gate_up_w, down_w, experts):
    normed_rows = rms_normed(hidden_rows, norm_gain)
    row_count, model_width = hidden_rows.shape
    top_count = route_ids.shape[-1]
    block_rows = min(BLOCK_ROWS, row_count)
    group_count = row_count // block_rows
    capacity = max(2, min(block_rows, block_rows * top_count // experts * 3 // 2))
    width = group_count * capacity
    groups = route_ids.reshape(group_count, block_rows, top_count)
    positions = slot_table(groups, experts, capacity)
    full_slot, part_slot, part_piece, pieces = wire_slots(experts, width)
    piece_width = model_width // pieces
    wire_rows = experts * SUBLANE

    hits_full = positions[:, :, None] == full_slot[None, None, :]
    hits_part = positions[:, :, None] == part_slot[None, None, :]
    pick_full = jnp.sum(hits_full.astype(jnp.int32), axis=1).astype(jnp.bfloat16).T
    pick_part = jnp.sum(hits_part.astype(jnp.int32), axis=1).astype(jnp.bfloat16).T
    send_full = jnp.dot(pick_full, normed_rows, preferred_element_type=jnp.float32)
    send_part = jnp.zeros((wire_rows, piece_width), jnp.float32)
    for piece in range(pieces):
        chosen = (part_piece == piece)[:, None]
        lanes = normed_rows[:, piece * piece_width:(piece + 1) * piece_width]
        send_part = send_part + jnp.dot(
            jnp.where(chosen, pick_part, jnp.zeros_like(pick_part)),
            lanes,
            preferred_element_type=jnp.float32,
        )
    outgoing = jnp.concatenate(
        [
            send_full.astype(jnp.bfloat16).reshape(experts, SUBLANE, model_width),
            send_part.astype(jnp.bfloat16).reshape(experts, SUBLANE, piece_width),
        ],
        axis=-1,
    )
    received = lax.all_to_all(outgoing, "expert", split_axis=0, concat_axis=0, tiled=True)

    extra = width - SUBLANE
    full_rows = received[:, :, :model_width].reshape(wire_rows, model_width)
    part_rows = received[:, :, model_width:].reshape(wire_rows, piece_width)
    joined_row = (
        jnp.arange(experts, dtype=jnp.int32)[:, None] * extra
        + jnp.arange(extra, dtype=jnp.int32)[None, :]
    ).reshape(-1)
    joined_count = experts * extra
    wire_joined = (
        jnp.arange(experts, dtype=jnp.int32)[:, None] * extra
        + jnp.arange(SUBLANE, dtype=jnp.int32)[None, :] % extra
    ).reshape(-1)
    gather_pieces = []
    spread = []
    for piece in range(pieces):
        table = (wire_joined[None, :] == joined_row[:, None]) & (part_piece == piece)[None, :]
        table = table.astype(jnp.bfloat16)
        spread.append(table)
        gather_pieces.append(
            jnp.dot(table, part_rows, preferred_element_type=jnp.float32).astype(jnp.bfloat16)
        )
    joined_rows = jnp.concatenate(gather_pieces, axis=-1)
    inputs = jnp.concatenate([full_rows, joined_rows], axis=0)
    gate_up = jnp.dot(inputs, gate_up_w, preferred_element_type=jnp.float32)
    ff = gate_up.shape[-1] // 2
    gate_sum, up_sum = gate_up[:, :ff], gate_up[:, ff:]
    hidden = (jax.nn.silu(gate_sum) * up_sum).astype(jnp.bfloat16)
    hidden = lax.optimization_barrier(hidden)
    result = jnp.dot(hidden, down_w, preferred_element_type=jnp.float32).astype(jnp.bfloat16)
    result_full = result[:wire_rows]
    result_joined = result[wire_rows:]
    back_part = jnp.zeros((wire_rows, piece_width), jnp.float32)
    for piece in range(pieces):
        back_part = back_part + jnp.dot(
            spread[piece].T,
            result_joined[:, piece * piece_width:(piece + 1) * piece_width],
            preferred_element_type=jnp.float32,
        )
    back = jnp.concatenate(
        [
            result_full.reshape(experts, SUBLANE, model_width),
            back_part.astype(jnp.bfloat16).reshape(experts, SUBLANE, piece_width),
        ],
        axis=-1,
    )
    returned = lax.all_to_all(back, "expert", split_axis=0, concat_axis=0, tiled=True)
    sent_back = back
    back_full = returned[:, :, :model_width].reshape(wire_rows, model_width)
    back_rows = returned[:, :, model_width:].reshape(wire_rows, piece_width)

    weights = combine[:, :, None]
    mix_full = jnp.sum(jnp.where(hits_full, weights, 0.0), axis=1)
    mix_part = jnp.sum(jnp.where(hits_part, weights, 0.0), axis=1)

    def split(mix):
        high = mix.astype(jnp.bfloat16)
        low = (mix - high.astype(jnp.float32)).astype(jnp.bfloat16)
        return [high, low]

    full_parts = split(mix_full)
    full_sum = jnp.dot(
        jnp.concatenate(full_parts, axis=0), back_full, preferred_element_type=jnp.float32
    )
    branch_full = full_sum[:row_count] + full_sum[row_count:]
    part_parts = []
    for piece in range(pieces):
        part_parts += split(jnp.where((part_piece == piece)[None, :], mix_part, 0.0))
    part_sum = jnp.dot(
        jnp.concatenate(part_parts, axis=0), back_rows, preferred_element_type=jnp.float32
    )
    branch_part = [
        part_sum[(2 * piece) * row_count:(2 * piece + 1) * row_count]
        + part_sum[(2 * piece + 1) * row_count:(2 * piece + 2) * row_count]
        for piece in range(pieces)
    ]
    branch_sum = branch_full + jnp.concatenate(branch_part, axis=-1)
    residual = hidden_rows.astype(jnp.float32)
    return (residual + branch_sum).astype(jnp.bfloat16), sent_back


def local(in_flight, entering, norm_gain, w_gate, w_up, w_down, routes, combine_weight):
    section_index = lax.axis_index("section")
    experts = lax.axis_size("expert") * w_gate.shape[1]
    carried = in_flight[0]
    gate_up_w = jnp.concatenate([w_gate[0, 0], w_up[0, 0]], axis=-1)
    traced = []
    step_routes = routes[0, 0]
    step_combine = combine_weight[0, 0]
    for tick_index in range(TICKS):
        layer_out, sent_back = apply_layer(
            carried,
            norm_gain[0],
            step_routes,
            step_combine,
            gate_up_w,
            w_down[0, 0],
            experts,
        )
        traced.append(layer_out)
        if tick_index + 1 < TICKS:
            _, step_routes, step_combine = lax.optimization_barrier(
                (sent_back, routes[0, tick_index + 1], combine_weight[0, tick_index + 1])
            )
            shifted = passed_along(layer_out, "section", 1)
            carried = jnp.where(section_index == 0, entering[tick_index], shifted)
    return jnp.stack(traced)[:, None]


def solution(mesh):
    placed = (
        P("section", "expert", None),
        P(None, "expert", None),
        P("section", None),
        P("section", "expert", None, None),
        P("section", "expert", None, None),
        P("section", "expert", None, None),
        P("section", None, "expert", None),
        P("section", None, "expert", None),
    )
    return jax.shard_map(
        local,
        mesh=mesh,
        in_specs=placed,
        out_specs=P(None, "section", "expert", None),
        check_vma=False,
    )
```

```python
import jax
import jax.numpy as jnp
from jax import lax
from jax.sharding import PartitionSpec as P

TICKS = 2


EPSILON = 1e-06
BLOCK_ROWS = 32
SUBLANE = 8


def passed_along(x, axis, by):
    devices = lax.axis_size(axis)
    pairs = [(i, i + by) for i in range(devices) if 0 <= i + by < devices]
    return lax.ppermute(x, axis, pairs)


def rms_normed(hidden_rows, norm_gain):
    as_float = hidden_rows.astype(jnp.float32)
    inv_scale = lax.rsqrt(jnp.mean(as_float * as_float, axis=-1, keepdims=True) + EPSILON)
    return (as_float * inv_scale * norm_gain.astype(jnp.float32)).astype(jnp.bfloat16)


def slot_table(route_ids, experts, capacity):
    group_count, row_count, top_count = route_ids.shape
    expert_marks = (route_ids[..., None] == jnp.arange(experts, dtype=jnp.int32)).astype(jnp.int32)
    expert_marks = expert_marks.reshape(group_count, row_count * top_count, experts)
    earlier_marks = jnp.cumsum(expert_marks, axis=1) - expert_marks
    slot_index = jnp.sum(earlier_marks * expert_marks, axis=-1).reshape(
        group_count, row_count, top_count
    )
    group_index = jnp.arange(group_count, dtype=jnp.int32)[:, None, None]
    group_width = group_count * capacity
    positions = route_ids * group_width + group_index * capacity + slot_index
    return positions.reshape(group_count * row_count, top_count)


def wire_slots(experts, width):
    extra = width - SUBLANE
    pieces = SUBLANE // extra
    row = jnp.arange(SUBLANE, dtype=jnp.int32)
    base = jnp.arange(experts, dtype=jnp.int32)[:, None] * width
    full_slot = (base + row[None, :]).reshape(-1)
    part_slot = (base + SUBLANE + row[None, :] % extra).reshape(-1)
    part_piece = jnp.broadcast_to(row[None, :] // extra, (experts, SUBLANE)).reshape(-1)
    return full_slot, part_slot, part_piece, pieces


def apply_layer(hidden_rows, norm_gain, route_ids, combine, gate_up_w, down_w, experts):
    normed_rows = rms_normed(hidden_rows, norm_gain)
    row_count, model_width = hidden_rows.shape
    top_count = route_ids.shape[-1]
    block_rows = min(BLOCK_ROWS, row_count)
    group_count = row_count // block_rows
    capacity = max(2, min(block_rows, block_rows * top_count // experts * 3 // 2))
    width = group_count * capacity
    groups = route_ids.reshape(group_count, block_rows, top_count)
    positions = slot_table(groups, experts, capacity)
    full_slot, part_slot, part_piece, pieces = wire_slots(experts, width)
    piece_width = model_width // pieces
    wire_rows = experts * SUBLANE

    hits_full = positions[:, :, None] == full_slot[None, None, :]
    hits_part = positions[:, :, None] == part_slot[None, None, :]
    pick_full = jnp.sum(hits_full.astype(jnp.int32), axis=1).astype(jnp.bfloat16).T
    pick_part = jnp.sum(hits_part.astype(jnp.int32), axis=1).astype(jnp.bfloat16).T
    send_full = jnp.dot(pick_full, normed_rows, preferred_element_type=jnp.float32)
    send_part = jnp.zeros((wire_rows, piece_width), jnp.float32)
    for piece in range(pieces):
        chosen = (part_piece == piece)[:, None]
        lanes = normed_rows[:, piece * piece_width:(piece + 1) * piece_width]
        send_part = send_part + jnp.dot(
            jnp.where(chosen, pick_part, jnp.zeros_like(pick_part)),
            lanes,
            preferred_element_type=jnp.float32,
        )
    outgoing = jnp.concatenate(
        [
            send_full.astype(jnp.bfloat16).reshape(experts, SUBLANE, model_width),
            send_part.astype(jnp.bfloat16).reshape(experts, SUBLANE, piece_width),
        ],
        axis=-1,
    )
    received = lax.all_to_all(outgoing, "expert", split_axis=0, concat_axis=0, tiled=True)

    extra = width - SUBLANE
    full_rows = received[:, :, :model_width].reshape(wire_rows, model_width)
    part_rows = received[:, :, model_width:].reshape(wire_rows, piece_width)
    joined_row = (
        jnp.arange(experts, dtype=jnp.int32)[:, None] * extra
        + jnp.arange(extra, dtype=jnp.int32)[None, :]
    ).reshape(-1)
    joined_count = experts * extra
    wire_joined = (
        jnp.arange(experts, dtype=jnp.int32)[:, None] * extra
        + jnp.arange(SUBLANE, dtype=jnp.int32)[None, :] % extra
    ).reshape(-1)
    spread = []
    for piece in range(pieces):
        table = (wire_joined[None, :] == joined_row[:, None]) & (part_piece == piece)[None, :]
        spread.append(table.astype(jnp.bfloat16))
    gathered = jnp.dot(
        jnp.concatenate(spread, axis=0), part_rows, preferred_element_type=jnp.float32
    ).astype(jnp.bfloat16)
    joined_rows = jnp.concatenate(
        [gathered[piece * joined_count:(piece + 1) * joined_count] for piece in range(pieces)],
        axis=-1,
    )
    inputs = jnp.concatenate([full_rows, joined_rows], axis=0)
    gate_up = jnp.dot(inputs, gate_up_w, preferred_element_type=jnp.float32)
    ff = gate_up.shape[-1] // 2
    gate_sum, up_sum = gate_up[:, :ff], gate_up[:, ff:]
    hidden = (jax.nn.silu(gate_sum) * up_sum).astype(jnp.bfloat16)
    hidden = lax.optimization_barrier(hidden)
    result = jnp.dot(hidden, down_w, preferred_element_type=jnp.float32).astype(jnp.bfloat16)
    result_full = result[:wire_rows]
    result_joined = result[wire_rows:]
    back_part = jnp.zeros((wire_rows, piece_width), jnp.float32)
    for piece in range(pieces):
        back_part = back_part + jnp.dot(
            spread[piece].T,
            result_joined[:, piece * piece_width:(piece + 1) * piece_width],
            preferred_element_type=jnp.float32,
        )
    back = jnp.concatenate(
        [
            result_full.reshape(experts, SUBLANE, model_width),
            back_part.astype(jnp.bfloat16).reshape(experts, SUBLANE, piece_width),
        ],
        axis=-1,
    )
    returned = lax.all_to_all(back, "expert", split_axis=0, concat_axis=0, tiled=True)
    sent_back = back
    back_full = returned[:, :, :model_width].reshape(wire_rows, model_width)
    back_rows = returned[:, :, model_width:].reshape(wire_rows, piece_width)

    weights = combine[:, :, None]
    mix_full = jnp.sum(jnp.where(hits_full, weights, 0.0), axis=1)
    mix_part = jnp.sum(jnp.where(hits_part, weights, 0.0), axis=1)

    def split(mix):
        high = mix.astype(jnp.bfloat16)
        low = (mix - high.astype(jnp.float32)).astype(jnp.bfloat16)
        return [high, low]

    full_parts = split(mix_full)
    full_sum = jnp.dot(
        jnp.concatenate(full_parts, axis=0), back_full, preferred_element_type=jnp.float32
    )
    branch_full = full_sum[:row_count] + full_sum[row_count:]
    part_parts = []
    for piece in range(pieces):
        part_parts += split(jnp.where((part_piece == piece)[None, :], mix_part, 0.0))
    part_sum = jnp.dot(
        jnp.concatenate(part_parts, axis=0), back_rows, preferred_element_type=jnp.float32
    )
    branch_part = [
        part_sum[(2 * piece) * row_count:(2 * piece + 1) * row_count]
        + part_sum[(2 * piece + 1) * row_count:(2 * piece + 2) * row_count]
        for piece in range(pieces)
    ]
    branch_sum = branch_full + jnp.concatenate(branch_part, axis=-1)
    residual = hidden_rows.astype(jnp.float32)
    return (residual + branch_sum).astype(jnp.bfloat16), sent_back


def local(in_flight, entering, norm_gain, w_gate, w_up, w_down, routes, combine_weight):
    section_index = lax.axis_index("section")
    experts = lax.axis_size("expert") * w_gate.shape[1]
    carried = in_flight[0]
    gate_up_w = jnp.concatenate([w_gate[0, 0], w_up[0, 0]], axis=-1)
    traced = []
    step_routes = routes[0, 0]
    step_combine = combine_weight[0, 0]
    for tick_index in range(TICKS):
        layer_out, sent_back = apply_layer(
            carried,
            norm_gain[0],
            step_routes,
            step_combine,
            gate_up_w,
            w_down[0, 0],
            experts,
        )
        traced.append(layer_out)
        if tick_index + 1 < TICKS:
            _, step_routes, step_combine = lax.optimization_barrier(
                (sent_back, routes[0, tick_index + 1], combine_weight[0, tick_index + 1])
            )
            shifted = passed_along(layer_out, "section", 1)
            carried = jnp.where(section_index == 0, entering[tick_index], shifted)
    return jnp.stack(traced)[:, None]


def solution(mesh):
    placed = (
        P("section", "expert", None),
        P(None, "expert", None),
        P("section", None),
        P("section", "expert", None, None),
        P("section", "expert", None, None),
        P("section", "expert", None, None),
        P("section", None, "expert", None),
        P("section", None, "expert", None),
    )
    return jax.shard_map(
        local,
        mesh=mesh,
        in_specs=placed,
        out_specs=P(None, "section", "expert", None),
        check_vma=False,
    )
```

```python
import jax
import jax.numpy as jnp
from jax import lax
from jax.sharding import PartitionSpec as P

TICKS = 2


EPSILON = 1e-06
BLOCK_ROWS = 32
SUBLANE = 8


def passed_along(x, axis, by):
    devices = lax.axis_size(axis)
    pairs = [(i, i + by) for i in range(devices) if 0 <= i + by < devices]
    return lax.ppermute(x, axis, pairs)


def rms_normed(hidden_rows, norm_gain):
    as_float = hidden_rows.astype(jnp.float32)
    inv_scale = lax.rsqrt(jnp.mean(as_float * as_float, axis=-1, keepdims=True) + EPSILON)
    return (as_float * inv_scale * norm_gain.astype(jnp.float32)).astype(jnp.bfloat16)


def slot_table(route_ids, experts, capacity):
    group_count, row_count, top_count = route_ids.shape
    expert_marks = (route_ids[..., None] == jnp.arange(experts, dtype=jnp.int32)).astype(jnp.int32)
    expert_marks = expert_marks.reshape(group_count, row_count * top_count, experts)
    earlier_marks = jnp.cumsum(expert_marks, axis=1) - expert_marks
    slot_index = jnp.sum(earlier_marks * expert_marks, axis=-1).reshape(
        group_count, row_count, top_count
    )
    group_index = jnp.arange(group_count, dtype=jnp.int32)[:, None, None]
    group_width = group_count * capacity
    positions = route_ids * group_width + group_index * capacity + slot_index
    return positions.reshape(group_count * row_count, top_count)


def wire_slots(experts, width):
    extra = width - SUBLANE
    pieces = SUBLANE // extra
    row = jnp.arange(SUBLANE, dtype=jnp.int32)
    base = jnp.arange(experts, dtype=jnp.int32)[:, None] * width
    full_slot = (base + row[None, :]).reshape(-1)
    part_slot = (base + SUBLANE + row[None, :] % extra).reshape(-1)
    part_piece = jnp.broadcast_to(row[None, :] // extra, (experts, SUBLANE)).reshape(-1)
    return full_slot, part_slot, part_piece, pieces


def apply_layer(hidden_rows, norm_gain, route_ids, combine, gate_up_w, down_w, experts, settle=False):
    normed_rows = rms_normed(hidden_rows, norm_gain)
    row_count, model_width = hidden_rows.shape
    top_count = route_ids.shape[-1]
    block_rows = min(BLOCK_ROWS, row_count)
    group_count = row_count // block_rows
    capacity = max(2, min(block_rows, block_rows * top_count // experts * 3 // 2))
    width = group_count * capacity
    groups = route_ids.reshape(group_count, block_rows, top_count)
    positions = slot_table(groups, experts, capacity)
    full_slot, part_slot, part_piece, pieces = wire_slots(experts, width)
    piece_width = model_width // pieces
    wire_rows = experts * SUBLANE

    hits_full = positions[:, :, None] == full_slot[None, None, :]
    hits_part = positions[:, :, None] == part_slot[None, None, :]
    pick_full = jnp.sum(hits_full.astype(jnp.int32), axis=1).astype(jnp.bfloat16).T
    pick_part = jnp.sum(hits_part.astype(jnp.int32), axis=1).astype(jnp.bfloat16).T
    send_full = jnp.dot(pick_full, normed_rows, preferred_element_type=jnp.float32)
    send_part = jnp.zeros((wire_rows, piece_width), jnp.float32)
    for piece in range(pieces):
        chosen = (part_piece == piece)[:, None]
        lanes = normed_rows[:, piece * piece_width:(piece + 1) * piece_width]
        send_part = send_part + jnp.dot(
            jnp.where(chosen, pick_part, jnp.zeros_like(pick_part)),
            lanes,
            preferred_element_type=jnp.float32,
        )
    outgoing = jnp.concatenate(
        [
            send_full.astype(jnp.bfloat16).reshape(experts, SUBLANE, model_width),
            send_part.astype(jnp.bfloat16).reshape(experts, SUBLANE, piece_width),
        ],
        axis=-1,
    )
    weights = combine[:, :, None]
    mix_full = jnp.sum(jnp.where(hits_full, weights, 0.0), axis=1)
    mix_part = jnp.sum(jnp.where(hits_part, weights, 0.0), axis=1)

    def split(mix):
        high = mix.astype(jnp.bfloat16)
        low = (mix - high.astype(jnp.float32)).astype(jnp.bfloat16)
        return [high, low]

    full_lhs = jnp.concatenate(split(mix_full), axis=0)
    part_parts = []
    for piece in range(pieces):
        part_parts += split(jnp.where((part_piece == piece)[None, :], mix_part, 0.0))
    part_lhs = jnp.concatenate(part_parts, axis=0)
    if settle:
        outgoing, full_lhs, part_lhs = lax.optimization_barrier((outgoing, full_lhs, part_lhs))
    received = lax.all_to_all(outgoing, "expert", split_axis=0, concat_axis=0, tiled=True)

    extra = width - SUBLANE
    full_rows = received[:, :, :model_width].reshape(wire_rows, model_width)
    part_rows = received[:, :, model_width:].reshape(wire_rows, piece_width)
    joined_row = (
        jnp.arange(experts, dtype=jnp.int32)[:, None] * extra
        + jnp.arange(extra, dtype=jnp.int32)[None, :]
    ).reshape(-1)
    joined_count = experts * extra
    wire_joined = (
        jnp.arange(experts, dtype=jnp.int32)[:, None] * extra
        + jnp.arange(SUBLANE, dtype=jnp.int32)[None, :] % extra
    ).reshape(-1)
    spread = []
    for piece in range(pieces):
        table = (wire_joined[None, :] == joined_row[:, None]) & (part_piece == piece)[None, :]
        spread.append(table.astype(jnp.bfloat16))
    gathered = jnp.dot(
        jnp.concatenate(spread, axis=0), part_rows, preferred_element_type=jnp.float32
    ).astype(jnp.bfloat16)
    joined_rows = jnp.concatenate(
        [gathered[piece * joined_count:(piece + 1) * joined_count] for piece in range(pieces)],
        axis=-1,
    )
    inputs = jnp.concatenate([full_rows, joined_rows], axis=0)
    gate_up = jnp.dot(inputs, gate_up_w, preferred_element_type=jnp.float32)
    ff = gate_up.shape[-1] // 2
    gate_sum, up_sum = gate_up[:, :ff], gate_up[:, ff:]
    hidden = (jax.nn.silu(gate_sum) * up_sum).astype(jnp.bfloat16)
    hidden = lax.optimization_barrier(hidden)
    result = jnp.dot(hidden, down_w, preferred_element_type=jnp.float32).astype(jnp.bfloat16)
    result_full = result[:wire_rows]
    result_joined = result[wire_rows:]
    back_part = jnp.zeros((wire_rows, piece_width), jnp.float32)
    for piece in range(pieces):
        back_part = back_part + jnp.dot(
            spread[piece].T,
            result_joined[:, piece * piece_width:(piece + 1) * piece_width],
            preferred_element_type=jnp.float32,
        )
    back = jnp.concatenate(
        [
            result_full.reshape(experts, SUBLANE, model_width),
            back_part.astype(jnp.bfloat16).reshape(experts, SUBLANE, piece_width),
        ],
        axis=-1,
    )
    if settle:
        back, full_lhs, part_lhs = lax.optimization_barrier((back, full_lhs, part_lhs))
    returned = lax.all_to_all(back, "expert", split_axis=0, concat_axis=0, tiled=True)
    sent_back = back
    back_full = returned[:, :, :model_width].reshape(wire_rows, model_width)
    back_rows = returned[:, :, model_width:].reshape(wire_rows, piece_width)

    full_sum = jnp.dot(full_lhs, back_full, preferred_element_type=jnp.float32)
    branch_full = full_sum[:row_count] + full_sum[row_count:]
    part_sum = jnp.dot(part_lhs, back_rows, preferred_element_type=jnp.float32)
    branch_part = [
        part_sum[(2 * piece) * row_count:(2 * piece + 1) * row_count]
        + part_sum[(2 * piece + 1) * row_count:(2 * piece + 2) * row_count]
        for piece in range(pieces)
    ]
    branch_sum = branch_full + jnp.concatenate(branch_part, axis=-1)
    residual = hidden_rows.astype(jnp.float32)
    return (residual + branch_sum).astype(jnp.bfloat16), sent_back


def local(in_flight, entering, norm_gain, w_gate, w_up, w_down, routes, combine_weight):
    section_index = lax.axis_index("section")
    experts = lax.axis_size("expert") * w_gate.shape[1]
    carried = in_flight[0]
    gate_up_w = jnp.concatenate([w_gate[0, 0], w_up[0, 0]], axis=-1)
    traced = []
    step_routes = routes[0, 0]
    step_combine = combine_weight[0, 0]
    for tick_index in range(TICKS):
        layer_out, sent_back = apply_layer(
            carried,
            norm_gain[0],
            step_routes,
            step_combine,
            gate_up_w,
            w_down[0, 0],
            experts,
            tick_index + 1 == TICKS,
        )
        traced.append(layer_out)
        if tick_index + 1 < TICKS:
            _, step_routes, step_combine = lax.optimization_barrier(
                (sent_back, routes[0, tick_index + 1], combine_weight[0, tick_index + 1])
            )
            shifted = passed_along(layer_out, "section", 1)
            carried = jnp.where(section_index == 0, entering[tick_index], shifted)
    return jnp.stack(traced)[:, None]


def solution(mesh):
    placed = (
        P("section", "expert", None),
        P(None, "expert", None),
        P("section", None),
        P("section", "expert", None, None),
        P("section", "expert", None, None),
        P("section", "expert", None, None),
        P("section", None, "expert", None),
        P("section", None, "expert", None),
    )
    return jax.shard_map(
        local,
        mesh=mesh,
        in_specs=placed,
        out_specs=P(None, "section", "expert", None),
        check_vma=False,
    )
```

```python
import jax
import jax.numpy as jnp
from jax import lax
from jax.sharding import PartitionSpec as P

TICKS = 2


EPSILON = 1e-06
BLOCK_ROWS = 32
SUBLANE = 8


def passed_along(x, axis, by):
    devices = lax.axis_size(axis)
    pairs = [(i, i + by) for i in range(devices) if 0 <= i + by < devices]
    return lax.ppermute(x, axis, pairs)


def rms_normed(hidden_rows, norm_gain):
    as_float = hidden_rows.astype(jnp.float32)
    inv_scale = lax.rsqrt(jnp.mean(as_float * as_float, axis=-1, keepdims=True) + EPSILON)
    return (as_float * inv_scale * norm_gain.astype(jnp.float32)).astype(jnp.bfloat16)


def slot_table(route_ids, experts, capacity):
    group_count, row_count, top_count = route_ids.shape
    expert_marks = (route_ids[..., None] == jnp.arange(experts, dtype=jnp.int32)).astype(jnp.int32)
    expert_marks = expert_marks.reshape(group_count, row_count * top_count, experts)
    earlier_marks = jnp.cumsum(expert_marks, axis=1) - expert_marks
    slot_index = jnp.sum(earlier_marks * expert_marks, axis=-1).reshape(
        group_count, row_count, top_count
    )
    group_index = jnp.arange(group_count, dtype=jnp.int32)[:, None, None]
    group_width = group_count * capacity
    positions = route_ids * group_width + group_index * capacity + slot_index
    return positions.reshape(group_count * row_count, top_count)


def wire_slots(experts, width):
    extra = width - SUBLANE
    pieces = SUBLANE // extra
    row = jnp.arange(SUBLANE, dtype=jnp.int32)
    base = jnp.arange(experts, dtype=jnp.int32)[:, None] * width
    full_slot = (base + row[None, :]).reshape(-1)
    part_slot = (base + SUBLANE + row[None, :] % extra).reshape(-1)
    part_piece = jnp.broadcast_to(row[None, :] // extra, (experts, SUBLANE)).reshape(-1)
    return full_slot, part_slot, part_piece, pieces


def step_tables(route_ids, combine, experts):
    row_count, top_count = route_ids.shape
    block_rows = min(BLOCK_ROWS, row_count)
    group_count = row_count // block_rows
    capacity = max(2, min(block_rows, block_rows * top_count // experts * 3 // 2))
    width = group_count * capacity
    positions = slot_table(route_ids.reshape(group_count, block_rows, top_count), experts, capacity)
    full_slot, part_slot, part_piece, pieces = wire_slots(experts, width)
    hits_full = positions[:, :, None] == full_slot[None, None, :]
    hits_part = positions[:, :, None] == part_slot[None, None, :]
    weights = combine[:, :, None]
    mix_full = jnp.sum(jnp.where(hits_full, weights, 0.0), axis=1)
    mix_part = jnp.sum(jnp.where(hits_part, weights, 0.0), axis=1)

    def split(mix):
        high = mix.astype(jnp.bfloat16)
        low = (mix - high.astype(jnp.float32)).astype(jnp.bfloat16)
        return [high, low]

    full_lhs = jnp.concatenate(split(mix_full), axis=0)
    part_parts = []
    for piece in range(pieces):
        part_parts += split(jnp.where((part_piece == piece)[None, :], mix_part, 0.0))
    pick_full = jnp.sum(hits_full.astype(jnp.int32), axis=1).astype(jnp.bfloat16).T
    pick_part = jnp.sum(hits_part.astype(jnp.int32), axis=1).astype(jnp.bfloat16).T
    return full_lhs, jnp.concatenate(part_parts, axis=0), pick_full, pick_part


def apply_layer(
    hidden_rows, norm_gain, route_ids, combine, gate_up_w, down_w, experts, settle=False,
    mix=None, carry=(),
):
    normed_rows = rms_normed(hidden_rows, norm_gain)
    row_count, model_width = hidden_rows.shape
    top_count = route_ids.shape[-1]
    block_rows = min(BLOCK_ROWS, row_count)
    group_count = row_count // block_rows
    capacity = max(2, min(block_rows, block_rows * top_count // experts * 3 // 2))
    width = group_count * capacity
    groups = route_ids.reshape(group_count, block_rows, top_count)
    positions = slot_table(groups, experts, capacity)
    full_slot, part_slot, part_piece, pieces = wire_slots(experts, width)
    piece_width = model_width // pieces
    wire_rows = experts * SUBLANE

    hits_full = positions[:, :, None] == full_slot[None, None, :]
    hits_part = positions[:, :, None] == part_slot[None, None, :]
    pick_full = jnp.sum(hits_full.astype(jnp.int32), axis=1).astype(jnp.bfloat16).T
    pick_part = jnp.sum(hits_part.astype(jnp.int32), axis=1).astype(jnp.bfloat16).T
    if mix is not None:
        pick_full, pick_part = mix[2], mix[3]
    send_full = jnp.dot(pick_full, normed_rows, preferred_element_type=jnp.float32)
    send_part = jnp.zeros((wire_rows, piece_width), jnp.float32)
    for piece in range(pieces):
        chosen = (part_piece == piece)[:, None]
        lanes = normed_rows[:, piece * piece_width:(piece + 1) * piece_width]
        send_part = send_part + jnp.dot(
            jnp.where(chosen, pick_part, jnp.zeros_like(pick_part)),
            lanes,
            preferred_element_type=jnp.float32,
        )
    outgoing = jnp.concatenate(
        [
            send_full.astype(jnp.bfloat16).reshape(experts, SUBLANE, model_width),
            send_part.astype(jnp.bfloat16).reshape(experts, SUBLANE, piece_width),
        ],
        axis=-1,
    )
    weights = combine[:, :, None]
    mix_full = jnp.sum(jnp.where(hits_full, weights, 0.0), axis=1)
    mix_part = jnp.sum(jnp.where(hits_part, weights, 0.0), axis=1)

    def split(mix):
        high = mix.astype(jnp.bfloat16)
        low = (mix - high.astype(jnp.float32)).astype(jnp.bfloat16)
        return [high, low]

    full_lhs = jnp.concatenate(split(mix_full), axis=0)
    part_parts = []
    for piece in range(pieces):
        part_parts += split(jnp.where((part_piece == piece)[None, :], mix_part, 0.0))
    part_lhs = jnp.concatenate(part_parts, axis=0)
    if mix is not None:
        full_lhs, part_lhs = mix[0], mix[1]
    if settle:
        outgoing, full_lhs, part_lhs = lax.optimization_barrier((outgoing, full_lhs, part_lhs))
    received = lax.all_to_all(outgoing, "expert", split_axis=0, concat_axis=0, tiled=True)

    extra = width - SUBLANE
    full_rows = received[:, :, :model_width].reshape(wire_rows, model_width)
    part_rows = received[:, :, model_width:].reshape(wire_rows, piece_width)
    joined_row = (
        jnp.arange(experts, dtype=jnp.int32)[:, None] * extra
        + jnp.arange(extra, dtype=jnp.int32)[None, :]
    ).reshape(-1)
    joined_count = experts * extra
    wire_joined = (
        jnp.arange(experts, dtype=jnp.int32)[:, None] * extra
        + jnp.arange(SUBLANE, dtype=jnp.int32)[None, :] % extra
    ).reshape(-1)
    spread = []
    for piece in range(pieces):
        table = (wire_joined[None, :] == joined_row[:, None]) & (part_piece == piece)[None, :]
        spread.append(table.astype(jnp.bfloat16))
    gathered = jnp.dot(
        jnp.concatenate(spread, axis=0), part_rows, preferred_element_type=jnp.float32
    ).astype(jnp.bfloat16)
    joined_rows = jnp.concatenate(
        [gathered[piece * joined_count:(piece + 1) * joined_count] for piece in range(pieces)],
        axis=-1,
    )
    inputs = jnp.concatenate([full_rows, joined_rows], axis=0)
    gate_up = jnp.dot(inputs, gate_up_w, preferred_element_type=jnp.float32)
    ff = gate_up.shape[-1] // 2
    gate_sum, up_sum = gate_up[:, :ff], gate_up[:, ff:]
    hidden = (jax.nn.silu(gate_sum) * up_sum).astype(jnp.bfloat16)
    hidden = lax.optimization_barrier(hidden)
    result = jnp.dot(hidden, down_w, preferred_element_type=jnp.float32).astype(jnp.bfloat16)
    result_full = result[:wire_rows]
    result_joined = result[wire_rows:]
    back_part = jnp.zeros((wire_rows, piece_width), jnp.float32)
    for piece in range(pieces):
        back_part = back_part + jnp.dot(
            spread[piece].T,
            result_joined[:, piece * piece_width:(piece + 1) * piece_width],
            preferred_element_type=jnp.float32,
        )
    back = jnp.concatenate(
        [
            result_full.reshape(experts, SUBLANE, model_width),
            back_part.astype(jnp.bfloat16).reshape(experts, SUBLANE, piece_width),
        ],
        axis=-1,
    )
    back, full_lhs, part_lhs, carry = lax.optimization_barrier((back, full_lhs, part_lhs, carry))
    returned = lax.all_to_all(back, "expert", split_axis=0, concat_axis=0, tiled=True)
    back_full = returned[:, :, :model_width].reshape(wire_rows, model_width)
    back_rows = returned[:, :, model_width:].reshape(wire_rows, piece_width)

    full_sum = jnp.dot(full_lhs, back_full, preferred_element_type=jnp.float32)
    branch_full = full_sum[:row_count] + full_sum[row_count:]
    part_sum = jnp.dot(part_lhs, back_rows, preferred_element_type=jnp.float32)
    branch_part = [
        part_sum[(2 * piece) * row_count:(2 * piece + 1) * row_count]
        + part_sum[(2 * piece + 1) * row_count:(2 * piece + 2) * row_count]
        for piece in range(pieces)
    ]
    branch_sum = branch_full + jnp.concatenate(branch_part, axis=-1)
    residual = hidden_rows.astype(jnp.float32)
    return (residual + branch_sum).astype(jnp.bfloat16), carry


def local(in_flight, entering, norm_gain, w_gate, w_up, w_down, routes, combine_weight):
    section_index = lax.axis_index("section")
    experts = lax.axis_size("expert") * w_gate.shape[1]
    carried = in_flight[0]
    gate_up_w = jnp.concatenate([w_gate[0, 0], w_up[0, 0]], axis=-1)
    traced = []
    step_mix = [None] + [
        step_tables(routes[0, t], combine_weight[0, t], experts) for t in range(1, TICKS)
    ]
    for tick_index in range(TICKS):
        layer_out, carry = apply_layer(
            carried,
            norm_gain[0],
            routes[0, tick_index],
            combine_weight[0, tick_index],
            gate_up_w,
            w_down[0, 0],
            experts,
            tick_index + 1 == TICKS,
            step_mix[tick_index],
            tuple(step_mix[tick_index + 1:]) if tick_index == 0 else (),
        )
        if tick_index == 0:
            step_mix = [None] + list(carry)
        traced.append(layer_out)
        if tick_index + 1 < TICKS:
            shifted = passed_along(layer_out, "section", 1)
            carried = jnp.where(section_index == 0, entering[tick_index], shifted)
    return jnp.stack(traced)[:, None]


def solution(mesh):
    placed = (
        P("section", "expert", None),
        P(None, "expert", None),
        P("section", None),
        P("section", "expert", None, None),
        P("section", "expert", None, None),
        P("section", "expert", None, None),
        P("section", None, "expert", None),
        P("section", None, "expert", None),
    )
    return jax.shard_map(
        local,
        mesh=mesh,
        in_specs=placed,
        out_specs=P(None, "section", "expert", None),
        check_vma=False,
    )
```
